128 devices in a mesh: dp: 32 (over z, x_lo, y), seq: 4 (over x_hi, core).
Axes of the slice: x: 4 (x_hi: 2, x_lo: 2; x = x_hi * 2 + x_lo), y: 4, z: 4, core: 2. Of those that a mesh axis runs over, the one named last changes fastest.
Arguments:
- queries: bfloat16 [32, 1024, 2560], P('dp', 'seq'), may hold values from -6 to 6
- keys_in: bfloat16 [32, 1024, 2560], P('dp', 'seq'), may hold values from -6 to 6
- values_in: bfloat16 [32, 1024, 2560], P('dp', 'seq'), may hold values from -6 to 6
- head_gain: float32 [20, 128], replicated, may hold values from 0.1 to 1.9
- master_weight: float32 [2560, 5120], P('dp', 'seq'), may hold values from -0.125 to 0.125
- gradient: float32 [2560, 5120], P('dp', 'seq'), may hold values from -6 to 6
- first_moment: float32 [2560, 5120], P('dp', 'seq'), may hold values from -4 to 4
- second_moment: float32 [2560, 5120], P('dp', 'seq'), may hold values from 0.01 to 4
Outputs:
- layer_out: bfloat16 [32, 1024, 5120], P('dp', 'seq')
- new_master: float32 [2560, 5120], P('dp', 'seq')
- new_first: float32 [2560, 5120], P('dp', 'seq')
- new_second: float32 [2560, 5120], P('dp', 'seq')
The draws below stay inside these ranges and needn't reach their ends.
All inputs are finite; a program needn't handle non-finite values.
Results may differ from the reference program's by a relative error of at most 0.0061.
Values may be sent and summed in bfloat16 or wider, within the bound.
No kernel may reach another device: no remote copies, remote signals or barrier semaphores. Data moves between devices by JAX's collectives and lax.ppermute only.
A program may use at most 192 MiB of HBM per device.

```python
import math
import jax
import jax.numpy as jnp
from jax import lax

D = 5120
HEAD = 128
H = 20
CH = 128
HD = 2560
LENGTH = 1024
SEQS = 32


def levels(key, dims, shards, least, high):
    level = 1.0
    for dim, shards_of in shards:
        draws = jax.random.uniform(jax.random.fold_in(jax.random.fold_in(key, 6), dim), (shards_of,), jnp.float32, least / len(shards), high / len(shards))
        level = level * jnp.repeat(jnp.exp(draws), dims[dim] // shards_of).reshape((-1,) + (1,) * (len(dims) - 1 - dim))
    return level


def scatter_about(stream_key, dims, spread, limit, cuts=(), dtype=jnp.bfloat16):
    values = spread * jax.random.normal(stream_key, dims, jnp.float32)
    if cuts:
        values = values * levels(stream_key, dims, cuts, -0.22, 0.18)
    return jnp.clip(values, -limit, limit).astype(dtype)


def setup_inputs(seed: int = 0) -> dict:
    seeds = jax.random.split(jax.random.key(seed), 9)
    return {
        "queries": scatter_about(seeds[0], (SEQS, LENGTH, HD), 1.0, 6.0, ((0, 32), (1, 4))),
        "keys_in": scatter_about(seeds[1], (SEQS, LENGTH, HD), 1.0, 6.0, ((0, 32), (1, 4))),
        "values_in": scatter_about(seeds[2], (SEQS, LENGTH, HD), 1.0, 6.0, ((0, 32), (1, 4))),
        "head_gain": jnp.clip(1.0 + 0.18 * jax.random.normal(seeds[3], (H, HEAD), jnp.float32), 0.1, 1.9),
        "master_weight": scatter_about(seeds[4], (HD, D), HD ** -0.5, 0.125, ((0, 32), (1, 4)), jnp.float32),
        "gradient": scatter_about(seeds[5], (HD, D), 1.0, 6.0, ((0, 32), (1, 4)), jnp.float32),
        "first_moment": scatter_about(seeds[6], (HD, D), 0.5, 4.0, ((0, 32), (1, 4)), jnp.float32),
        "second_moment": jnp.clip(jnp.exp(math.log(4.0) - 5.9914646 * jax.random.uniform(seeds[7], (HD, D), jnp.float32) ** levels(seeds[7], (HD, D), ((0, 32), (1, 4)), -0.2, 0.2)), 0.01, 4.0),
    }


beta_one = 0.9
beta_two = 0.95
learn_rate = 0.0003
decay_rate = 0.1
adam_eps = 1e-08
step_count = 100
norm_eps = 1e-06

def featurize(block, seq_length):
    positions = jnp.arange(block.shape[0]).astype(jnp.float32)
    angles = positions * (math.pi / (2.0 * seq_length))
    rectified = jnp.maximum(block.astype(jnp.float32), 0.0)
    cosine = rectified * jnp.cos(angles)[:, None, None]
    sine = rectified * jnp.sin(angles)[:, None, None]
    return jnp.concatenate([cosine, sine], axis=2).astype(jnp.bfloat16)

def one_sequence(query_seq, key_seq, value_seq, head_gain):
    seq_length = query_seq.shape[0]
    query_heads = query_seq.reshape(seq_length, H, HEAD)
    key_heads = key_seq.reshape(seq_length, H, HEAD)
    value_heads = value_seq.reshape(seq_length, H, HEAD)
    query_feat = featurize(query_heads, seq_length).astype(jnp.float32)
    key_feat = featurize(key_heads, seq_length).astype(jnp.float32)
    blocks = seq_length // CH
    query_blocks = query_feat.reshape(blocks, CH, H, 2 * HEAD)
    key_blocks = key_feat.reshape(blocks, CH, H, 2 * HEAD)
    value_blocks = value_heads.astype(jnp.float32).reshape(blocks, CH, H, HEAD)
    scores = jnp.einsum('cihf,cjhf->chij', query_blocks, key_blocks)
    causal_mask = jnp.arange(CH)[:, None] >= jnp.arange(CH)[None, :]
    scores = jnp.where(causal_mask[None, None], scores, 0.0).astype(jnp.bfloat16)
    inside_block = jnp.einsum('chij,cjhe->cihe', scores.astype(jnp.float32), value_blocks)
    states = jnp.einsum('cjhf,cjhe->chfe', key_blocks, value_blocks)
    running = jnp.cumsum(states, axis=0)
    before = jnp.concatenate([jnp.zeros_like(states[:1]), running[:-1]], axis=0).astype(jnp.bfloat16)
    from_before = jnp.einsum('cihf,chfe->cihe', query_blocks, before.astype(jnp.float32))
    attended = (inside_block + from_before).reshape(seq_length, H, HEAD)
    mean_square = lax.optimization_barrier(jnp.mean(attended * attended, axis=2, keepdims=True))
    normed = (attended * lax.rsqrt(mean_square + norm_eps) * head_gain[None]).astype(jnp.bfloat16)
    return normed.reshape(seq_length, H * HEAD)

def reference(queries, keys_in, values_in, head_gain, master_weight, gradient, first_moment, second_moment):
    new_first = beta_one * first_moment + (1.0 - beta_one) * gradient
    new_second = beta_two * second_moment + (1.0 - beta_two) * gradient * gradient
    corrected = new_first / (1.0 - beta_one ** step_count) / (jnp.sqrt(new_second / (1.0 - beta_two ** step_count)) + adam_eps)
    new_master = master_weight - learn_rate * (corrected + decay_rate * master_weight)
    proj = new_master.astype(jnp.bfloat16)

    def per_sequence(items):
        normed = one_sequence(items[0], items[1], items[2], head_gain)
        return jnp.dot(normed, proj, preferred_element_type=jnp.float32).astype(jnp.bfloat16)
    layer_out = lax.map(per_sequence, (queries, keys_in, values_in))
    return (layer_out, new_master, new_first, new_second)
```

```python
import math

import jax
import jax.numpy as jnp
from jax import lax
from jax.sharding import PartitionSpec as P

HEAD = 128
H = 20
CH = 128


beta_one = 0.9
beta_two = 0.95
learn_rate = 0.0003
decay_rate = 0.1
adam_eps = 1e-08
step_count = 100
norm_eps = 1e-06


def featurize(block, seq_length):
    positions = jnp.arange(block.shape[0], dtype=jnp.int32).astype(jnp.float32)
    angles = positions * (math.pi / (2.0 * seq_length))
    rectified = jnp.maximum(block.astype(jnp.float32), 0.0)
    cosine = rectified * jnp.cos(angles)[:, None, None]
    sine = rectified * jnp.sin(angles)[:, None, None]
    return jnp.concatenate([cosine, sine], axis=2).astype(jnp.bfloat16)


def block_states(key_feat, value_heads):
    blocks = key_feat.shape[0] // CH
    key_blocks = key_feat.reshape(blocks, CH, key_feat.shape[1], key_feat.shape[2])
    value_blocks = value_heads.reshape(blocks, CH, value_heads.shape[1], value_heads.shape[2])
    return jnp.einsum(
        "cjhf,cjhe->chfe", key_blocks, value_blocks, preferred_element_type=jnp.float32
    )


def attend(query_feat, key_feat, value_heads, states):
    count = query_feat.shape[0]
    heads_here = query_feat.shape[1]
    blocks = count // CH
    query_blocks = query_feat.reshape(blocks, CH, heads_here, 2 * HEAD)
    key_blocks = key_feat.reshape(blocks, CH, heads_here, 2 * HEAD)
    value_blocks = value_heads.reshape(blocks, CH, heads_here, HEAD)
    scores = jnp.einsum(
        "cihf,cjhf->chij", query_blocks, key_blocks, preferred_element_type=jnp.float32
    )
    causal_mask = jnp.arange(CH)[:, None] >= jnp.arange(CH)[None, :]
    scores = jnp.where(causal_mask[None, None], scores, 0.0).astype(jnp.bfloat16)
    inside_block = jnp.einsum(
        "chij,cjhe->cihe", scores, value_blocks, preferred_element_type=jnp.float32
    )
    running = jnp.cumsum(states, axis=0)
    before = jnp.concatenate([jnp.zeros_like(states[:1]), running[:-1]], axis=0)
    before = before.astype(jnp.bfloat16)
    from_before = jnp.einsum(
        "cihf,chfe->cihe", query_blocks, before, preferred_element_type=jnp.float32
    )
    return (inside_block + from_before).reshape(count, heads_here, HEAD)


def normalize(attended, gain_rows):
    mean_square = jnp.mean(attended * attended, axis=2, keepdims=True)
    return (attended * lax.rsqrt(mean_square + norm_eps) * gain_rows[None]).astype(jnp.bfloat16)


def on_device(
    queries, keys_in, values_in, head_gain, master_weight, gradient, first_moment, second_moment
):
    moment_one = beta_one * first_moment + (1.0 - beta_one) * gradient
    moment_two = beta_two * second_moment + (1.0 - beta_two) * gradient * gradient
    corrected = (
        moment_one
        / (1.0 - beta_one**step_count)
        / (jnp.sqrt(moment_two / (1.0 - beta_two**step_count)) + adam_eps)
    )
    updated = master_weight - learn_rate * (corrected + decay_rate * master_weight)
    weights = updated.astype(jnp.bfloat16)
    tokens_here = queries.shape[1]
    seq_length = tokens_here * lax.axis_size("seq")
    query_heads = queries[0].reshape(tokens_here, H, HEAD)
    key_heads = keys_in[0].reshape(tokens_here, H, HEAD)
    value_heads = values_in[0].reshape(tokens_here, H, HEAD)
    query_group, key_group, value_group = (
        lax.all_to_all(query_heads, "seq", split_axis=1, concat_axis=0, tiled=True),
        lax.all_to_all(key_heads, "seq", split_axis=1, concat_axis=0, tiled=True),
        lax.all_to_all(value_heads, "seq", split_axis=1, concat_axis=0, tiled=True),
    )
    heads_here = query_group.shape[1]
    query_feat = featurize(query_group, seq_length)
    key_feat = featurize(key_group, seq_length)
    states = block_states(key_feat, value_group)
    attended = attend(query_feat, key_feat, value_group, states)
    gain_rows = lax.dynamic_slice_in_dim(
        head_gain, lax.axis_index("seq") * heads_here, heads_here, 0
    )
    normed_group = normalize(attended, gain_rows)
    normed_all = lax.all_gather(normed_group, "seq", axis=1, tiled=True)
    normed_all = normed_all.reshape(normed_all.shape[0], H * HEAD)
    cols = lax.all_gather(weights, "dp", axis=0, tiled=True)
    part = jnp.dot(normed_all, cols, preferred_element_type=jnp.float32).astype(jnp.bfloat16)
    projected = lax.all_to_all(part, "seq", split_axis=0, concat_axis=1, tiled=True)
    layer_out = projected[None]
    return (layer_out, updated, moment_one, moment_two)


def solution(mesh):
    in_specs = (
        P("dp", "seq", None),
        P("dp", "seq", None),
        P("dp", "seq", None),
        P(),
        P("dp", "seq"),
        P("dp", "seq"),
        P("dp", "seq"),
        P("dp", "seq"),
    )
    out_specs = (P("dp", "seq", None), P("dp", "seq"), P("dp", "seq"), P("dp", "seq"))
    return jax.shard_map(
        on_device, mesh=mesh, in_specs=in_specs, out_specs=out_specs, check_vma=False
    )
```

```python
import math

import jax
import jax.numpy as jnp
from jax import lax
from jax.sharding import Mesh, PartitionSpec as P

HEAD = 128
DP = ("z", "xl", "y")
SEQ = ("xh", "c")
H = 20
CH = 128


beta_one = 0.9
beta_two = 0.95
learn_rate = 0.0003
decay_rate = 0.1
adam_eps = 1e-08
step_count = 100
norm_eps = 1e-06


def ring_gather(x, axis, size):
    index = lax.axis_index(axis)
    if size == 2:
        other = lax.ppermute(x, axis, [(0, 1), (1, 0)])
        stacked = jnp.stack([x, other])
    else:
        forward = [(k, (k + 1) % size) for k in range(size)]
        backward = [(k, (k - 1) % size) for k in range(size)]
        from_left = lax.ppermute(x, axis, forward)
        from_right = lax.ppermute(x, axis, backward)
        half = x.shape[0] // 2
        far = jnp.concatenate(
            [
                lax.ppermute(from_left[:half], axis, forward),
                lax.ppermute(from_right[half:], axis, backward),
            ],
            axis=0,
        )
        stacked = jnp.stack([x, from_left, far, from_right])
    order = (index - jnp.arange(size)) % size
    return jnp.take(stacked, order, axis=0)


def gather_rows(weights):
    width = weights.shape[1] // 2
    pieces = []
    for first, second in (("y", "z"), ("z", "y")):
        part = weights[:, width * len(pieces) : width * (len(pieces) + 1)]
        part = ring_gather(part, "xl", 2)
        part = ring_gather(part, first, 4)
        part = ring_gather(part, second, 4)
        if first == "y":
            part = jnp.transpose(part, (0, 2, 1, 3, 4))
        else:
            part = jnp.transpose(part, (1, 2, 0, 3, 4))
        pieces.append(part.reshape(-1, width))
    return jnp.concatenate(pieces, axis=1)


def featurize(block, seq_length):
    positions = jnp.arange(block.shape[0], dtype=jnp.int32).astype(jnp.float32)
    angles = positions * (math.pi / (2.0 * seq_length))
    rectified = jnp.maximum(block.astype(jnp.float32), 0.0)
    cosine = rectified * jnp.cos(angles)[:, None, None]
    sine = rectified * jnp.sin(angles)[:, None, None]
    return jnp.concatenate([cosine, sine], axis=2).astype(jnp.bfloat16)


def block_states(key_feat, value_heads):
    blocks = key_feat.shape[0] // CH
    key_blocks = key_feat.reshape(blocks, CH, key_feat.shape[1], key_feat.shape[2])
    value_blocks = value_heads.reshape(blocks, CH, value_heads.shape[1], value_heads.shape[2])
    return jnp.einsum(
        "cjhf,cjhe->chfe", key_blocks, value_blocks, preferred_element_type=jnp.float32
    )


def attend(query_feat, key_feat, value_heads, states):
    count = query_feat.shape[0]
    heads_here = query_feat.shape[1]
    blocks = count // CH
    query_blocks = query_feat.reshape(blocks, CH, heads_here, 2 * HEAD)
    key_blocks = key_feat.reshape(blocks, CH, heads_here, 2 * HEAD)
    value_blocks = value_heads.reshape(blocks, CH, heads_here, HEAD)
    scores = jnp.einsum(
        "cihf,cjhf->chij", query_blocks, key_blocks, preferred_element_type=jnp.float32
    )
    causal_mask = jnp.arange(CH)[:, None] >= jnp.arange(CH)[None, :]
    scores = jnp.where(causal_mask[None, None], scores, 0.0).astype(jnp.bfloat16)
    inside_block = jnp.einsum(
        "chij,cjhe->cihe", scores, value_blocks, preferred_element_type=jnp.float32
    )
    running = jnp.cumsum(states, axis=0)
    before = jnp.concatenate([jnp.zeros_like(states[:1]), running[:-1]], axis=0)
    before = before.astype(jnp.bfloat16)
    from_before = jnp.einsum(
        "cihf,chfe->cihe", query_blocks, before, preferred_element_type=jnp.float32
    )
    return (inside_block + from_before).reshape(count, heads_here, HEAD)


def normalize(attended, gain_rows):
    mean_square = jnp.mean(attended * attended, axis=2, keepdims=True)
    return (attended * lax.rsqrt(mean_square + norm_eps) * gain_rows[None]).astype(jnp.bfloat16)


def on_device(
    queries, keys_in, values_in, head_gain, master_weight, gradient, first_moment, second_moment
):
    moment_one = beta_one * first_moment + (1.0 - beta_one) * gradient
    moment_two = beta_two * second_moment + (1.0 - beta_two) * gradient * gradient
    corrected = (
        moment_one
        / (1.0 - beta_one**step_count)
        / (jnp.sqrt(moment_two / (1.0 - beta_two**step_count)) + adam_eps)
    )
    updated = master_weight - learn_rate * (corrected + decay_rate * master_weight)
    weights = updated.astype(jnp.bfloat16)
    tokens_here = queries.shape[1]
    seq_length = tokens_here * lax.axis_size(SEQ)
    query_heads = queries[0].reshape(tokens_here, H, HEAD)
    key_heads = keys_in[0].reshape(tokens_here, H, HEAD)
    value_heads = values_in[0].reshape(tokens_here, H, HEAD)
    query_group, key_group, value_group = (
        lax.all_to_all(query_heads, SEQ, split_axis=1, concat_axis=0, tiled=True),
        lax.all_to_all(key_heads, SEQ, split_axis=1, concat_axis=0, tiled=True),
        lax.all_to_all(value_heads, SEQ, split_axis=1, concat_axis=0, tiled=True),
    )
    heads_here = query_group.shape[1]
    query_feat = featurize(query_group, seq_length)
    key_feat = featurize(key_group, seq_length)
    states = block_states(key_feat, value_group)
    attended = attend(query_feat, key_feat, value_group, states)
    gain_rows = lax.dynamic_slice_in_dim(
        head_gain, lax.axis_index(SEQ) * heads_here, heads_here, 0
    )
    normed_group = normalize(attended, gain_rows)
    normed_all = lax.all_gather(normed_group, SEQ, axis=1, tiled=True)
    normed_all = normed_all.reshape(normed_all.shape[0], H * HEAD)
    cols = gather_rows(weights)
    part = jnp.dot(normed_all, cols, preferred_element_type=jnp.float32).astype(jnp.bfloat16)
    projected = lax.all_to_all(part, SEQ, split_axis=0, concat_axis=1, tiled=True)
    layer_out = projected[None]
    return (layer_out, updated, moment_one, moment_two)


def solution(mesh):
    fine = Mesh(mesh.devices.reshape(4, 2, 4, 2, 2), DP + SEQ)
    data = P(DP, SEQ, None)
    blocks = P(DP, SEQ)
    in_specs = (data, data, data, P(), blocks, blocks, blocks, blocks)
    out_specs = (data, blocks, blocks, blocks)
    return jax.shard_map(
        on_device, mesh=fine, in_specs=in_specs, out_specs=out_specs, check_vma=False
    )
```

```python
import math

import jax
import jax.numpy as jnp
from jax import lax
from jax.sharding import Mesh, PartitionSpec as P

HEAD = 128
DP = ("z", "xl", "y")
SEQ = ("xh", "c")
H = 20
CH = 128


beta_one = 0.9
beta_two = 0.95
learn_rate = 0.0003
decay_rate = 0.1
adam_eps = 1e-08
step_count = 100
norm_eps = 1e-06


def ring_send(x, axis, size):
    if size == 2:
        return (lax.ppermute(x, axis, [(0, 1), (1, 0)]),)
    forward = [(k, (k + 1) % size) for k in range(size)]
    backward = [(k, (k - 1) % size) for k in range(size)]
    return (lax.ppermute(x, axis, forward), lax.ppermute(x, axis, backward))


def ring_far(received, axis, size):
    if size == 2:
        return received
    forward = [(k, (k + 1) % size) for k in range(size)]
    backward = [(k, (k - 1) % size) for k in range(size)]
    from_left, from_right = received
    half = from_left.shape[0] // 2
    far = jnp.concatenate(
        [
            lax.ppermute(from_left[:half], axis, forward),
            lax.ppermute(from_right[half:], axis, backward),
        ],
        axis=0,
    )
    return (from_left, far, from_right)


def ring_finish(x, received, axis, size):
    index = lax.axis_index(axis)
    stacked = jnp.stack((x,) + tuple(received))
    order = (index - jnp.arange(size)) % size
    return jnp.take(stacked, order, axis=0)


def ring_gather(x, axis, size):
    return ring_finish(x, ring_far(ring_send(x, axis, size), axis, size), axis, size)


STAGES = (("y", "z"), ("z", "y"))


def gather_start(weights):
    width = weights.shape[1] // 2
    parts = []
    for number, (first, _) in enumerate(STAGES):
        part = weights[:, width * number : width * (number + 1)]
        part = ring_gather(part, "xl", 2)
        parts.append(ring_gather(part, first, 4))
    return parts


def gather_finish(parts, sent):
    pieces = []
    for part, received, (first, second) in zip(parts, sent, STAGES):
        part = ring_finish(part, received, second, 4)
        if first == "y":
            part = jnp.transpose(part, (0, 2, 1, 3, 4))
        else:
            part = jnp.transpose(part, (1, 2, 0, 3, 4))
        pieces.append(part.reshape(-1, part.shape[-1]))
    return jnp.concatenate(pieces, axis=1)

def featurize(block, seq_length):
    positions = jnp.arange(block.shape[0], dtype=jnp.int32).astype(jnp.float32)
    angles = positions * (math.pi / (2.0 * seq_length))
    rectified = jnp.maximum(block.astype(jnp.float32), 0.0)
    cosine = rectified * jnp.cos(angles)[:, None, None]
    sine = rectified * jnp.sin(angles)[:, None, None]
    return jnp.concatenate([cosine, sine], axis=2).astype(jnp.bfloat16)


def block_states(key_feat, value_heads):
    blocks = key_feat.shape[0] // CH
    key_blocks = key_feat.reshape(blocks, CH, key_feat.shape[1], key_feat.shape[2])
    value_blocks = value_heads.reshape(blocks, CH, value_heads.shape[1], value_heads.shape[2])
    return jnp.einsum(
        "cjhf,cjhe->chfe", key_blocks, value_blocks, preferred_element_type=jnp.float32
    )


def attend(query_feat, key_feat, value_heads, states):
    count = query_feat.shape[0]
    heads_here = query_feat.shape[1]
    blocks = count // CH
    query_blocks = query_feat.reshape(blocks, CH, heads_here, 2 * HEAD)
    key_blocks = key_feat.reshape(blocks, CH, heads_here, 2 * HEAD)
    value_blocks = value_heads.reshape(blocks, CH, heads_here, HEAD)
    scores = jnp.einsum(
        "cihf,cjhf->chij", query_blocks, key_blocks, preferred_element_type=jnp.float32
    )
    causal_mask = jnp.arange(CH)[:, None] >= jnp.arange(CH)[None, :]
    scores = jnp.where(causal_mask[None, None], scores, 0.0).astype(jnp.bfloat16)
    inside_block = jnp.einsum(
        "chij,cjhe->cihe", scores, value_blocks, preferred_element_type=jnp.float32
    )
    running = jnp.cumsum(states, axis=0)
    before = jnp.concatenate([jnp.zeros_like(states[:1]), running[:-1]], axis=0)
    before = before.astype(jnp.bfloat16)
    from_before = jnp.einsum(
        "cihf,chfe->cihe", query_blocks, before, preferred_element_type=jnp.float32
    )
    return (inside_block + from_before).reshape(count, heads_here, HEAD)


def normalize(attended, gain_rows):
    mean_square = jnp.mean(attended * attended, axis=2, keepdims=True)
    return (attended * lax.rsqrt(mean_square + norm_eps) * gain_rows[None]).astype(jnp.bfloat16)


def on_device(
    queries, keys_in, values_in, head_gain, master_weight, gradient, first_moment, second_moment
):
    moment_one = beta_one * first_moment + (1.0 - beta_one) * gradient
    moment_two = beta_two * second_moment + (1.0 - beta_two) * gradient * gradient
    corrected = (
        moment_one
        / (1.0 - beta_one**step_count)
        / (jnp.sqrt(moment_two / (1.0 - beta_two**step_count)) + adam_eps)
    )
    updated = master_weight - learn_rate * (corrected + decay_rate * master_weight)
    weights = updated.astype(jnp.bfloat16)
    tokens_here = queries.shape[1]
    seq_length = tokens_here * lax.axis_size(SEQ)
    parts = gather_start(weights)
    parts, query_heads = lax.optimization_barrier(
        (parts, queries[0].reshape(tokens_here, H, HEAD))
    )
    query_group = lax.all_to_all(query_heads, SEQ, split_axis=1, concat_axis=0, tiled=True)
    sent = [ring_send(part, second, 4) for part, (_, second) in zip(parts, STAGES)]
    sent, key_heads = lax.optimization_barrier((sent, keys_in[0].reshape(tokens_here, H, HEAD)))
    key_group = lax.all_to_all(key_heads, SEQ, split_axis=1, concat_axis=0, tiled=True)
    sent = [ring_far(received, second, 4) for received, (_, second) in zip(sent, STAGES)]
    sent, value_heads = lax.optimization_barrier(
        (sent, values_in[0].reshape(tokens_here, H, HEAD))
    )
    value_group = lax.all_to_all(value_heads, SEQ, split_axis=1, concat_axis=0, tiled=True)
    heads_here = query_group.shape[1]
    query_feat = featurize(query_group, seq_length)
    key_feat = featurize(key_group, seq_length)
    states = block_states(key_feat, value_group)
    attended = attend(query_feat, key_feat, value_group, states)
    gain_rows = lax.dynamic_slice_in_dim(
        head_gain, lax.axis_index(SEQ) * heads_here, heads_here, 0
    )
    normed_group = normalize(attended, gain_rows)
    normed_all = lax.all_gather(normed_group, SEQ, axis=1, tiled=True)
    normed_all = normed_all.reshape(normed_all.shape[0], H * HEAD)
    cols = gather_finish(parts, sent)
    part = jnp.dot(normed_all, cols, preferred_element_type=jnp.float32).astype(jnp.bfloat16)
    projected = lax.all_to_all(part, SEQ, split_axis=0, concat_axis=1, tiled=True)
    layer_out = projected[None]
    return (layer_out, updated, moment_one, moment_two)


def solution(mesh):
    fine = Mesh(mesh.devices.reshape(4, 2, 4, 2, 2), DP + SEQ)
    data = P(DP, SEQ, None)
    blocks = P(DP, SEQ)
    in_specs = (data, data, data, P(), blocks, blocks, blocks, blocks)
    out_specs = (data, blocks, blocks, blocks)
    return jax.shard_map(
        on_device, mesh=fine, in_specs=in_specs, out_specs=out_specs, check_vma=False
    )
```

```python
import math

import jax
import jax.numpy as jnp
from jax import lax
from jax.sharding import Mesh, PartitionSpec as P

HEAD = 128
DP = ("z", "xl", "y")
SEQ = ("xh", "c")
H = 20
CH = 128


beta_one = 0.9
beta_two = 0.95
learn_rate = 0.0003
decay_rate = 0.1
adam_eps = 1e-08
step_count = 100
norm_eps = 1e-06


def ring_send(x, axis, size):
    if size == 2:
        return (lax.ppermute(x, axis, [(0, 1), (1, 0)]),)
    forward = [(k, (k + 1) % size) for k in range(size)]
    backward = [(k, (k - 1) % size) for k in range(size)]
    return (lax.ppermute(x, axis, forward), lax.ppermute(x, axis, backward))


def ring_far(received, axis, size):
    if size == 2:
        return received
    forward = [(k, (k + 1) % size) for k in range(size)]
    backward = [(k, (k - 1) % size) for k in range(size)]
    from_left, from_right = received
    half = from_left.shape[0] // 2
    far = jnp.concatenate(
        [
            lax.ppermute(from_left[:half], axis, forward),
            lax.ppermute(from_right[half:], axis, backward),
        ],
        axis=0,
    )
    return (from_left, far, from_right)


def ring_finish(x, received):
    return jnp.stack((x,) + tuple(received))


def ring_gather(x, axis, size):
    return ring_finish(x, ring_far(ring_send(x, axis, size), axis, size))


STAGES = (("y", "z"), ("z", "y"))


def gather_start(weights):
    width = weights.shape[1] // 2
    parts = []
    for number, (first, _) in enumerate(STAGES):
        part = weights[:, width * number : width * (number + 1)]
        part = ring_gather(part, "xl", 2)
        parts.append(ring_gather(part, first, 4))
    return parts


def gather_finish(parts, sent, heads_order):
    z = lax.axis_index("z")
    xl = lax.axis_index("xl")
    y = lax.axis_index("y")
    blocks_per_group = 8
    target = jnp.arange(32)
    group = heads_order[target // blocks_per_group]
    absolute = group * blocks_per_group + target % blocks_per_group
    z_rel = (z - absolute // 8) % 4
    xl_rel = (xl - (absolute // 4) % 2) % 2
    y_rel = (y - absolute % 4) % 4
    pieces = []
    for part, received, (first, _) in zip(parts, sent, STAGES):
        part = ring_finish(part, received)
        if first == "y":
            source = z_rel * 8 + y_rel * 2 + xl_rel
        else:
            source = y_rel * 8 + z_rel * 2 + xl_rel
        flat = part.reshape((32,) + part.shape[3:])
        pieces.append(jnp.take(flat, source, axis=0).reshape(-1, part.shape[-1]))
    return jnp.concatenate(pieces, axis=1)


def seq_shift(x, shift):
    return lax.ppermute(x, SEQ, [(k, (k + shift) % 4) for k in range(4)])

def featurize(block, seq_length):
    positions = jnp.arange(block.shape[0], dtype=jnp.int32).astype(jnp.float32)
    angles = positions * (math.pi / (2.0 * seq_length))
    rectified = jnp.maximum(block.astype(jnp.float32), 0.0)
    cosine = rectified * jnp.cos(angles)[:, None, None]
    sine = rectified * jnp.sin(angles)[:, None, None]
    return jnp.concatenate([cosine, sine], axis=2).astype(jnp.bfloat16)


def block_states(key_feat, value_heads):
    blocks = key_feat.shape[0] // CH
    key_blocks = key_feat.reshape(blocks, CH, key_feat.shape[1], key_feat.shape[2])
    value_blocks = value_heads.reshape(blocks, CH, value_heads.shape[1], value_heads.shape[2])
    return jnp.einsum(
        "cjhf,cjhe->chfe", key_blocks, value_blocks, preferred_element_type=jnp.float32
    )


def attend(query_feat, key_feat, value_heads, states):
    count = query_feat.shape[0]
    heads_here = query_feat.shape[1]
    blocks = count // CH
    query_blocks = query_feat.reshape(blocks, CH, heads_here, 2 * HEAD)
    key_blocks = key_feat.reshape(blocks, CH, heads_here, 2 * HEAD)
    value_blocks = value_heads.reshape(blocks, CH, heads_here, HEAD)
    scores = jnp.einsum(
        "cihf,cjhf->chij", query_blocks, key_blocks, preferred_element_type=jnp.float32
    )
    causal_mask = jnp.arange(CH)[:, None] >= jnp.arange(CH)[None, :]
    scores = jnp.where(causal_mask[None, None], scores, 0.0).astype(jnp.bfloat16)
    inside_block = jnp.einsum(
        "chij,cjhe->cihe", scores, value_blocks, preferred_element_type=jnp.float32
    )
    running = jnp.cumsum(states, axis=0)
    before = jnp.concatenate([jnp.zeros_like(states[:1]), running[:-1]], axis=0)
    before = before.astype(jnp.bfloat16)
    from_before = jnp.einsum(
        "cihf,chfe->cihe", query_blocks, before, preferred_element_type=jnp.float32
    )
    return (inside_block + from_before).reshape(count, heads_here, HEAD)


def normalize(attended, gain_rows):
    mean_square = jnp.mean(attended * attended, axis=2, keepdims=True)
    return (attended * lax.rsqrt(mean_square + norm_eps) * gain_rows[None]).astype(jnp.bfloat16)


def on_device(
    queries, keys_in, values_in, head_gain, master_weight, gradient, first_moment, second_moment
):
    moment_one = beta_one * first_moment + (1.0 - beta_one) * gradient
    moment_two = beta_two * second_moment + (1.0 - beta_two) * gradient * gradient
    corrected = (
        moment_one
        / (1.0 - beta_one**step_count)
        / (jnp.sqrt(moment_two / (1.0 - beta_two**step_count)) + adam_eps)
    )
    updated = master_weight - learn_rate * (corrected + decay_rate * master_weight)
    weights = updated.astype(jnp.bfloat16)
    tokens_here = queries.shape[1]
    seq_length = tokens_here * lax.axis_size(SEQ)
    parts = gather_start(weights)
    parts, query_heads = lax.optimization_barrier(
        (parts, queries[0].reshape(tokens_here, H, HEAD))
    )
    query_group = lax.all_to_all(query_heads, SEQ, split_axis=1, concat_axis=0, tiled=True)
    sent = [ring_send(part, second, 4) for part, (_, second) in zip(parts, STAGES)]
    sent, key_heads = lax.optimization_barrier((sent, keys_in[0].reshape(tokens_here, H, HEAD)))
    key_group = lax.all_to_all(key_heads, SEQ, split_axis=1, concat_axis=0, tiled=True)
    sent = [ring_far(received, second, 4) for received, (_, second) in zip(sent, STAGES)]
    sent, value_heads = lax.optimization_barrier(
        (sent, values_in[0].reshape(tokens_here, H, HEAD))
    )
    value_group = lax.all_to_all(value_heads, SEQ, split_axis=1, concat_axis=0, tiled=True)
    heads_here = query_group.shape[1]
    query_feat = featurize(query_group, seq_length)
    key_feat = featurize(key_group, seq_length)
    states = block_states(key_feat, value_group)
    attended = attend(query_feat, key_feat, value_group, states)
    gain_rows = lax.dynamic_slice_in_dim(
        head_gain, lax.axis_index(SEQ) * heads_here, heads_here, 0
    )
    normed_group = normalize(attended, gain_rows)
    seq_index = lax.axis_index(SEQ)
    flat_group = normed_group.reshape(normed_group.shape[0], heads_here * HEAD)
    normed_all = jnp.concatenate(
        [flat_group] + [seq_shift(flat_group, shift) for shift in (1, 2, 3)], axis=1
    )
    heads_order = (seq_index - jnp.arange(4)) % 4
    cols = gather_finish(parts, sent, heads_order)
    outputs = []
    for shift in (2, 1, 3, 0):
        chunk = lax.dynamic_slice_in_dim(
            normed_all, ((seq_index + shift) % 4) * tokens_here, tokens_here, 0
        )
        part = jnp.dot(chunk, cols, preferred_element_type=jnp.float32).astype(jnp.bfloat16)
        outputs.append((shift, part if shift == 0 else seq_shift(part, shift)))
    by_shift = jnp.stack([part for _, part in sorted(outputs, key=lambda item: item[0])])
    projected = jnp.take(by_shift, (seq_index - jnp.arange(4)) % 4, axis=0)
    projected = jnp.transpose(projected, (1, 0, 2)).reshape(tokens_here, -1)
    layer_out = projected[None]
    return (layer_out, updated, moment_one, moment_two)


def solution(mesh):
    fine = Mesh(mesh.devices.reshape(4, 2, 4, 2, 2), DP + SEQ)
    data = P(DP, SEQ, None)
    blocks = P(DP, SEQ)
    in_specs = (data, data, data, P(), blocks, blocks, blocks, blocks)
    out_specs = (data, blocks, blocks, blocks)
    return jax.shard_map(
        on_device, mesh=fine, in_specs=in_specs, out_specs=out_specs, check_vma=False
    )
```

```python
import math

import jax
import jax.numpy as jnp
from jax import lax
from jax.sharding import Mesh, PartitionSpec as P

HEAD = 128
DP = ("z", "xl", "y")
SEQ = ("xh", "c")
H = 20
CH = 128


beta_one = 0.9
beta_two = 0.95
learn_rate = 0.0003
decay_rate = 0.1
adam_eps = 1e-08
step_count = 100
norm_eps = 1e-06


def ring_send(x, axis, size):
    if size == 2:
        return (lax.ppermute(x, axis, [(0, 1), (1, 0)]),)
    forward = [(k, (k + 1) % size) for k in range(size)]
    backward = [(k, (k - 1) % size) for k in range(size)]
    return (lax.ppermute(x, axis, forward), lax.ppermute(x, axis, backward))


def ring_far(received, axis, size):
    if size == 2:
        return received
    forward = [(k, (k + 1) % size) for k in range(size)]
    backward = [(k, (k - 1) % size) for k in range(size)]
    from_left, from_right = received
    half = from_left.shape[0] // 2
    far = jnp.concatenate(
        [
            lax.ppermute(from_left[:half], axis, forward),
            lax.ppermute(from_right[half:], axis, backward),
        ],
        axis=0,
    )
    return (from_left, far, from_right)


def ring_finish(x, received):
    return jnp.stack((x,) + tuple(received))


def ring_gather(x, axis, size):
    return ring_finish(x, ring_far(ring_send(x, axis, size), axis, size))


STAGES = (("y", "z"), ("z", "y"))


def gather_start(weights):
    width = weights.shape[1] // 2
    parts = []
    for number, (first, _) in enumerate(STAGES):
        part = weights[:, width * number : width * (number + 1)]
        part = ring_gather(part, "xl", 2)
        parts.append(ring_gather(part, first, 4))
    return parts


def gather_finish(parts, sent, heads_order):
    z = lax.axis_index("z")
    xl = lax.axis_index("xl")
    y = lax.axis_index("y")
    blocks_per_group = 8
    target = jnp.arange(32)
    group = heads_order[target // blocks_per_group]
    absolute = group * blocks_per_group + target % blocks_per_group
    z_rel = (z - absolute // 8) % 4
    xl_rel = (xl - (absolute // 4) % 2) % 2
    y_rel = (y - absolute % 4) % 4
    pieces = []
    for part, received, (first, _) in zip(parts, sent, STAGES):
        part = ring_finish(part, received)
        if first == "y":
            source = z_rel * 8 + y_rel * 2 + xl_rel
        else:
            source = y_rel * 8 + z_rel * 2 + xl_rel
        flat = part.reshape((32,) + part.shape[3:])
        pieces.append(jnp.take(flat, source, axis=0).reshape(-1, part.shape[-1]))
    return jnp.concatenate(pieces, axis=1)


def seq_shift(x, shift):
    return lax.ppermute(x, SEQ, [(k, (k + shift) % 4) for k in range(4)])

def featurize(block, offset, seq_length):
    positions = (offset + jnp.arange(block.shape[0], dtype=jnp.int32)).astype(jnp.float32)
    angles = positions * (math.pi / (2.0 * seq_length))
    rectified = jnp.maximum(block.astype(jnp.float32), 0.0)
    cosine = rectified * jnp.cos(angles)[:, None, None]
    sine = rectified * jnp.sin(angles)[:, None, None]
    return jnp.concatenate([cosine, sine], axis=2).astype(jnp.bfloat16)


def to_blocks(x):
    return x.reshape((x.shape[0] // CH, CH) + x.shape[1:])


def normalize(attended, gain_rows):
    mean_square = jnp.mean(attended * attended, axis=2, keepdims=True)
    return (attended * lax.rsqrt(mean_square + norm_eps) * gain_rows[None]).astype(jnp.bfloat16)


def swap(x, axis):
    return lax.ppermute(x, axis, [(0, 1), (1, 0)])


def on_device(
    queries, keys_in, values_in, head_gain, master_weight, gradient, first_moment, second_moment
):
    moment_one = beta_one * first_moment + (1.0 - beta_one) * gradient
    moment_two = beta_two * second_moment + (1.0 - beta_two) * gradient * gradient
    corrected = (
        moment_one
        / (1.0 - beta_one**step_count)
        / (jnp.sqrt(moment_two / (1.0 - beta_two**step_count)) + adam_eps)
    )
    updated = master_weight - learn_rate * (corrected + decay_rate * master_weight)
    weights = updated.astype(jnp.bfloat16)
    tokens_here = queries.shape[1]
    seq_length = tokens_here * lax.axis_size(SEQ)
    half = lax.axis_index("xh")
    core = lax.axis_index("c")
    heads_here = H // 2
    parts = gather_start(weights)
    parts, query_heads = lax.optimization_barrier(
        (parts, queries[0].reshape(tokens_here, H, HEAD))
    )
    query_group = lax.all_to_all(query_heads, "c", split_axis=1, concat_axis=0, tiled=True)
    sent = [ring_send(part, second, 4) for part, (_, second) in zip(parts, STAGES)]
    sent, key_heads = lax.optimization_barrier((sent, keys_in[0].reshape(tokens_here, H, HEAD)))
    key_group = lax.all_to_all(key_heads, "c", split_axis=1, concat_axis=0, tiled=True)
    sent = [ring_far(received, second, 4) for received, (_, second) in zip(sent, STAGES)]
    sent, value_heads = lax.optimization_barrier(
        (sent, values_in[0].reshape(tokens_here, H, HEAD))
    )
    value_group = lax.all_to_all(value_heads, "c", split_axis=1, concat_axis=0, tiled=True)
    span = query_group.shape[0]
    offset = half * span
    query_blocks = to_blocks(featurize(query_group, offset, seq_length))
    key_blocks = to_blocks(featurize(key_group, offset, seq_length))
    value_blocks = to_blocks(value_group)
    states = jnp.einsum(
        "cjhf,cjhe->chfe", key_blocks, value_blocks, preferred_element_type=jnp.float32
    )
    chip_total = jnp.sum(states, axis=0)
    earlier = lax.ppermute(chip_total, "xh", [(0, 1)])
    scores = jnp.einsum(
        "cihf,cjhf->chij", query_blocks, key_blocks, preferred_element_type=jnp.float32
    )
    causal_mask = jnp.arange(CH)[:, None] >= jnp.arange(CH)[None, :]
    scores = jnp.where(causal_mask[None, None], scores, 0.0).astype(jnp.bfloat16)
    inside_block = jnp.einsum(
        "chij,cjhe->cihe", scores, value_blocks, preferred_element_type=jnp.float32
    )
    running = jnp.cumsum(states, axis=0)
    local_before = jnp.concatenate([jnp.zeros_like(states[:1]), running[:-1]], axis=0)
    before = (earlier[None] + local_before).astype(jnp.bfloat16)
    from_before = jnp.einsum(
        "cihf,chfe->cihe", query_blocks, before, preferred_element_type=jnp.float32
    )
    attended = (inside_block + from_before).reshape(span, heads_here, HEAD)
    gain_rows = lax.dynamic_slice_in_dim(head_gain, core * heads_here, heads_here, 0)
    normed_group = normalize(attended, gain_rows)
    normed_own = lax.all_to_all(normed_group, "c", split_axis=0, concat_axis=1, tiled=True)
    normed_own = normed_own.reshape(tokens_here, H * HEAD)
    normed_peer = swap(normed_own, "xh")
    mine = gather_finish(parts, sent, jnp.arange(4))
    partner = swap(mine, "c")
    tokens = jnp.concatenate([normed_peer, normed_own], axis=0)
    wide = jnp.concatenate(
        [
            jnp.dot(tokens, mine, preferred_element_type=jnp.float32),
            jnp.dot(tokens, partner, preferred_element_type=jnp.float32),
        ],
        axis=1,
    ).astype(jnp.bfloat16)
    returned = swap(wide[:tokens_here], "xh")
    by_offset = jnp.stack(
        [
            wide[tokens_here:, : wide.shape[1] // 2],
            wide[tokens_here:, wide.shape[1] // 2 :],
            returned[:, : wide.shape[1] // 2],
            returned[:, wide.shape[1] // 2 :],
        ]
    )
    block = jnp.arange(4)
    offsets = ((block // 2 - half) % 2) * 2 + (block % 2 - core) % 2
    projected = jnp.take(by_offset, offsets, axis=0)
    projected = jnp.transpose(projected, (1, 0, 2)).reshape(tokens_here, -1)
    layer_out = projected[None]
    return (layer_out, updated, moment_one, moment_two)


def solution(mesh):
    fine = Mesh(mesh.devices.reshape(4, 2, 4, 2, 2), DP + SEQ)
    data = P(DP, SEQ, None)
    blocks = P(DP, SEQ)
    in_specs = (data, data, data, P(), blocks, blocks, blocks, blocks)
    out_specs = (data, blocks, blocks, blocks)
    return jax.shard_map(
        on_device, mesh=fine, in_specs=in_specs, out_specs=out_specs, check_vma=False
    )
```

```python
import math

import jax
import jax.numpy as jnp
from jax import lax
from jax.sharding import Mesh, PartitionSpec as P

HEAD = 128
DP = ("z", "xl", "y")
SEQ = ("xh", "c")
H = 20
CH = 128


beta_one = 0.9
beta_two = 0.95
learn_rate = 0.0003
decay_rate = 0.1
adam_eps = 1e-08
step_count = 100
norm_eps = 1e-06


def ring_send(x, axis, size):
    if size == 2:
        return (lax.ppermute(x, axis, [(0, 1), (1, 0)]),)
    forward = [(k, (k + 1) % size) for k in range(size)]
    backward = [(k, (k - 1) % size) for k in range(size)]
    return (lax.ppermute(x, axis, forward), lax.ppermute(x, axis, backward))


def ring_far(received, axis, size):
    if size == 2:
        return received
    forward = [(k, (k + 1) % size) for k in range(size)]
    backward = [(k, (k - 1) % size) for k in range(size)]
    from_left, from_right = received
    half = from_left.shape[0] // 2
    far = jnp.concatenate(
        [
            lax.ppermute(from_left[:half], axis, forward),
            lax.ppermute(from_right[half:], axis, backward),
        ],
        axis=0,
    )
    return (from_left, far, from_right)


def ring_finish(x, received):
    return jnp.stack((x,) + tuple(received))


def ring_gather(x, axis, size):
    return ring_finish(x, ring_far(ring_send(x, axis, size), axis, size))


STAGES = (("y", "z"), ("z", "y"))


def gather_start(weights):
    width = weights.shape[1] // 2
    parts = []
    for number, (first, _) in enumerate(STAGES):
        part = weights[:, width * number : width * (number + 1)]
        part = ring_gather(part, "xl", 2)
        parts.append(ring_gather(part, first, 4))
    return parts


def gather_finish(parts, sent, heads_order):
    z = lax.axis_index("z")
    xl = lax.axis_index("xl")
    y = lax.axis_index("y")
    blocks_per_group = 8
    target = jnp.arange(32)
    group = heads_order[target // blocks_per_group]
    absolute = group * blocks_per_group + target % blocks_per_group
    z_rel = (z - absolute // 8) % 4
    xl_rel = (xl - (absolute // 4) % 2) % 2
    y_rel = (y - absolute % 4) % 4
    pieces = []
    for part, received, (first, _) in zip(parts, sent, STAGES):
        part = ring_finish(part, received)
        if first == "y":
            source = z_rel * 8 + y_rel * 2 + xl_rel
        else:
            source = y_rel * 8 + z_rel * 2 + xl_rel
        flat = part.reshape((32,) + part.shape[3:])
        pieces.append(jnp.take(flat, source, axis=0).reshape(-1, part.shape[-1]))
    return jnp.concatenate(pieces, axis=1)


def seq_shift(x, shift):
    return lax.ppermute(x, SEQ, [(k, (k + shift) % 4) for k in range(4)])

def featurize(block, offset, seq_length):
    positions = (offset + jnp.arange(block.shape[0], dtype=jnp.int32)).astype(jnp.float32)
    angles = positions * (math.pi / (2.0 * seq_length))
    rectified = jnp.maximum(block.astype(jnp.float32), 0.0)
    cosine = rectified * jnp.cos(angles)[:, None, None]
    sine = rectified * jnp.sin(angles)[:, None, None]
    return jnp.concatenate([cosine, sine], axis=2).astype(jnp.bfloat16)


def to_blocks(x):
    return x.reshape((x.shape[0] // CH, CH) + x.shape[1:])


def normalize(attended, gain_rows):
    mean_square = jnp.mean(attended * attended, axis=2, keepdims=True)
    return (attended * lax.rsqrt(mean_square + norm_eps) * gain_rows[None]).astype(jnp.bfloat16)


def swap(x, axis):
    return lax.ppermute(x, axis, [(0, 1), (1, 0)])


def pair_exchange(x, core, keep_axis, join_axis):
    size = x.shape[keep_axis] // 2
    mine = lax.dynamic_slice_in_dim(x, core * size, size, keep_axis)
    theirs = lax.dynamic_slice_in_dim(x, (1 - core) * size, size, keep_axis)
    received = swap(theirs, "c")
    return jnp.where(
        core == 0,
        jnp.concatenate([mine, received], axis=join_axis),
        jnp.concatenate([received, mine], axis=join_axis),
    )


def on_device(
    queries, keys_in, values_in, head_gain, master_weight, gradient, first_moment, second_moment
):
    moment_one = beta_one * first_moment + (1.0 - beta_one) * gradient
    moment_two = beta_two * second_moment + (1.0 - beta_two) * gradient * gradient
    corrected = (
        moment_one
        / (1.0 - beta_one**step_count)
        / (jnp.sqrt(moment_two / (1.0 - beta_two**step_count)) + adam_eps)
    )
    updated = master_weight - learn_rate * (corrected + decay_rate * master_weight)
    weights = updated.astype(jnp.bfloat16)
    tokens_here = queries.shape[1]
    seq_length = tokens_here * lax.axis_size(SEQ)
    half = lax.axis_index("xh")
    core = lax.axis_index("c")
    heads_here = H // 2
    parts = gather_start(weights)
    parts, query_heads = lax.optimization_barrier(
        (parts, queries[0].reshape(tokens_here, H, HEAD))
    )
    query_group = pair_exchange(query_heads, core, 1, 0)
    sent = [ring_send(part, second, 4) for part, (_, second) in zip(parts, STAGES)]
    sent, key_heads = lax.optimization_barrier((sent, keys_in[0].reshape(tokens_here, H, HEAD)))
    key_group = pair_exchange(key_heads, core, 1, 0)
    sent = [ring_far(received, second, 4) for received, (_, second) in zip(sent, STAGES)]
    sent, value_heads = lax.optimization_barrier(
        (sent, values_in[0].reshape(tokens_here, H, HEAD))
    )
    value_group = pair_exchange(value_heads, core, 1, 0)
    span = query_group.shape[0]
    offset = half * span
    query_blocks = to_blocks(featurize(query_group, offset, seq_length))
    key_blocks = to_blocks(featurize(key_group, offset, seq_length))
    value_blocks = to_blocks(value_group)
    states = jnp.einsum(
        "cjhf,cjhe->chfe", key_blocks, value_blocks, preferred_element_type=jnp.float32
    )
    chip_total = jnp.sum(states, axis=0)
    earlier = lax.ppermute(chip_total, "xh", [(0, 1)])
    scores = jnp.einsum(
        "cihf,cjhf->chij", query_blocks, key_blocks, preferred_element_type=jnp.float32
    )
    causal_mask = jnp.arange(CH)[:, None] >= jnp.arange(CH)[None, :]
    scores = jnp.where(causal_mask[None, None], scores, 0.0).astype(jnp.bfloat16)
    inside_block = jnp.einsum(
        "chij,cjhe->cihe", scores, value_blocks, preferred_element_type=jnp.float32
    )
    running = jnp.cumsum(states, axis=0)
    local_before = jnp.concatenate([jnp.zeros_like(states[:1]), running[:-1]], axis=0)
    before = (earlier[None] + local_before).astype(jnp.bfloat16)
    from_before = jnp.einsum(
        "cihf,chfe->cihe", query_blocks, before, preferred_element_type=jnp.float32
    )
    attended = (inside_block + from_before).reshape(span, heads_here, HEAD)
    gain_rows = lax.dynamic_slice_in_dim(head_gain, core * heads_here, heads_here, 0)
    normed_group = normalize(attended, gain_rows)
    normed_own = pair_exchange(normed_group, core, 0, 1)
    normed_own = normed_own.reshape(tokens_here, H * HEAD)
    normed_peer = swap(normed_own, "xh")
    mine = gather_finish(parts, sent, jnp.arange(4))
    partner = swap(mine, "c")
    peer_wide = jnp.concatenate(
        [
            jnp.dot(normed_peer, mine, preferred_element_type=jnp.float32),
            jnp.dot(normed_peer, partner, preferred_element_type=jnp.float32),
        ],
        axis=1,
    ).astype(jnp.bfloat16)
    returned = swap(peer_wide, "xh")
    own_wide = jnp.concatenate(
        [
            jnp.dot(normed_own, mine, preferred_element_type=jnp.float32),
            jnp.dot(normed_own, partner, preferred_element_type=jnp.float32),
        ],
        axis=1,
    ).astype(jnp.bfloat16)
    width = own_wide.shape[1] // 2
    by_offset = jnp.stack(
        [
            own_wide[:, :width],
            own_wide[:, width:],
            returned[:, :width],
            returned[:, width:],
        ]
    )
    block = jnp.arange(4)
    offsets = ((block // 2 - half) % 2) * 2 + (block % 2 - core) % 2
    projected = jnp.take(by_offset, offsets, axis=0)
    projected = jnp.transpose(projected, (1, 0, 2)).reshape(tokens_here, -1)
    layer_out = projected[None]
    return (layer_out, updated, moment_one, moment_two)


def solution(mesh):
    fine = Mesh(mesh.devices.reshape(4, 2, 4, 2, 2), DP + SEQ)
    data = P(DP, SEQ, None)
    blocks = P(DP, SEQ)
    in_specs = (data, data, data, P(), blocks, blocks, blocks, blocks)
    out_specs = (data, blocks, blocks, blocks)
    return jax.shard_map(
        on_device, mesh=fine, in_specs=in_specs, out_specs=out_specs, check_vma=False
    )
```

```python
import math

import jax
import jax.numpy as jnp
from jax import lax
from jax.sharding import Mesh, PartitionSpec as P

HEAD = 128
DP = ("z", "xl", "y")
SEQ = ("xh", "c")
H = 20
CH = 128


beta_one = 0.9
beta_two = 0.95
learn_rate = 0.0003
decay_rate = 0.1
adam_eps = 1e-08
step_count = 100
norm_eps = 1e-06


def ring_send(x, axis, size):
    if size == 2:
        return (lax.ppermute(x, axis, [(0, 1), (1, 0)]),)
    forward = [(k, (k + 1) % size) for k in range(size)]
    backward = [(k, (k - 1) % size) for k in range(size)]
    return (lax.ppermute(x, axis, forward), lax.ppermute(x, axis, backward))


def ring_far(received, axis, size):
    if size == 2:
        return received
    forward = [(k, (k + 1) % size) for k in range(size)]
    backward = [(k, (k - 1) % size) for k in range(size)]
    from_left, from_right = received
    half = from_left.shape[0] // 2
    far = jnp.concatenate(
        [
            lax.ppermute(from_left[:half], axis, forward),
            lax.ppermute(from_right[half:], axis, backward),
        ],
        axis=0,
    )
    return (from_left, far, from_right)


def ring_finish(x, received):
    return jnp.stack((x,) + tuple(received))


def ring_gather(x, axis, size):
    return ring_finish(x, ring_far(ring_send(x, axis, size), axis, size))


STAGES = (("y", "z"), ("z", "y"))


def gather_start(weights):
    width = weights.shape[1] // 2
    parts = []
    for number, (first, _) in enumerate(STAGES):
        part = weights[:, width * number : width * (number + 1)]
        part = ring_gather(part, "xl", 2)
        parts.append(ring_gather(part, first, 4))
    return parts


def gather_finish(parts, sent, heads_order):
    z = lax.axis_index("z")
    xl = lax.axis_index("xl")
    y = lax.axis_index("y")
    blocks_per_group = 8
    target = jnp.arange(32)
    group = heads_order[target // blocks_per_group]
    absolute = group * blocks_per_group + target % blocks_per_group
    z_rel = (z - absolute // 8) % 4
    xl_rel = (xl - (absolute // 4) % 2) % 2
    y_rel = (y - absolute % 4) % 4
    pieces = []
    for part, received, (first, _) in zip(parts, sent, STAGES):
        part = ring_finish(part, received)
        if first == "y":
            source = z_rel * 8 + y_rel * 2 + xl_rel
        else:
            source = y_rel * 8 + z_rel * 2 + xl_rel
        flat = part.reshape((32,) + part.shape[3:])
        pieces.append(jnp.take(flat, source, axis=0).reshape(-1, part.shape[-1]))
    return jnp.concatenate(pieces, axis=1)


def seq_shift(x, shift):
    return lax.ppermute(x, SEQ, [(k, (k + shift) % 4) for k in range(4)])

def featurize(block, offset, seq_length):
    positions = (offset + jnp.arange(block.shape[0], dtype=jnp.int32)).astype(jnp.float32)
    angles = positions * (math.pi / (2.0 * seq_length))
    rectified = jnp.maximum(block.astype(jnp.float32), 0.0)
    cosine = rectified * jnp.cos(angles)[:, None, None]
    sine = rectified * jnp.sin(angles)[:, None, None]
    return jnp.concatenate([cosine, sine], axis=2).astype(jnp.bfloat16)


def to_blocks(x):
    return x.reshape((x.shape[0] // CH, CH) + x.shape[1:])


def normalize(attended, gain_rows):
    mean_square = jnp.mean(attended * attended, axis=2, keepdims=True)
    return (attended * lax.rsqrt(mean_square + norm_eps) * gain_rows[None]).astype(jnp.bfloat16)


def swap(x, axis):
    return lax.ppermute(x, axis, [(0, 1), (1, 0)])


def pair_exchange(x, core, keep_axis, join_axis):
    size = x.shape[keep_axis] // 2
    mine = lax.dynamic_slice_in_dim(x, core * size, size, keep_axis)
    theirs = lax.dynamic_slice_in_dim(x, (1 - core) * size, size, keep_axis)
    received = swap(theirs, "c")
    return jnp.where(
        core == 0,
        jnp.concatenate([mine, received], axis=join_axis),
        jnp.concatenate([received, mine], axis=join_axis),
    )


def on_device(
    queries, keys_in, values_in, head_gain, master_weight, gradient, first_moment, second_moment
):
    moment_one = beta_one * first_moment + (1.0 - beta_one) * gradient
    moment_two = beta_two * second_moment + (1.0 - beta_two) * gradient * gradient
    corrected = (
        moment_one
        / (1.0 - beta_one**step_count)
        / (jnp.sqrt(moment_two / (1.0 - beta_two**step_count)) + adam_eps)
    )
    updated = master_weight - learn_rate * (corrected + decay_rate * master_weight)
    weights = updated.astype(jnp.bfloat16)
    tokens_here = queries.shape[1]
    seq_length = tokens_here * lax.axis_size(SEQ)
    half = lax.axis_index("xh")
    core = lax.axis_index("c")
    heads_here = H // 2
    both = jnp.concatenate([weights, swap(weights, "xh")], axis=1)
    parts = gather_start(both)
    parts, query_heads = lax.optimization_barrier(
        (parts, queries[0].reshape(tokens_here, H, HEAD))
    )
    query_group = pair_exchange(query_heads, core, 1, 0)
    sent = [ring_send(part, second, 4) for part, (_, second) in zip(parts, STAGES)]
    sent, key_heads = lax.optimization_barrier((sent, keys_in[0].reshape(tokens_here, H, HEAD)))
    key_group = pair_exchange(key_heads, core, 1, 0)
    sent = [ring_far(received, second, 4) for received, (_, second) in zip(sent, STAGES)]
    sent, value_heads = lax.optimization_barrier(
        (sent, values_in[0].reshape(tokens_here, H, HEAD))
    )
    value_group = pair_exchange(value_heads, core, 1, 0)
    span = query_group.shape[0]
    offset = half * span
    query_blocks = to_blocks(featurize(query_group, offset, seq_length))
    key_blocks = to_blocks(featurize(key_group, offset, seq_length))
    value_blocks = to_blocks(value_group)
    states = jnp.einsum(
        "cjhf,cjhe->chfe", key_blocks, value_blocks, preferred_element_type=jnp.float32
    )
    chip_total = jnp.sum(states, axis=0)
    earlier = lax.ppermute(chip_total, "xh", [(0, 1)])
    scores = jnp.einsum(
        "cihf,cjhf->chij", query_blocks, key_blocks, preferred_element_type=jnp.float32
    )
    causal_mask = jnp.arange(CH)[:, None] >= jnp.arange(CH)[None, :]
    scores = jnp.where(causal_mask[None, None], scores, 0.0).astype(jnp.bfloat16)
    inside_block = jnp.einsum(
        "chij,cjhe->cihe", scores, value_blocks, preferred_element_type=jnp.float32
    )
    running = jnp.cumsum(states, axis=0)
    local_before = jnp.concatenate([jnp.zeros_like(states[:1]), running[:-1]], axis=0)
    before = (earlier[None] + local_before).astype(jnp.bfloat16)
    from_before = jnp.einsum(
        "cihf,chfe->cihe", query_blocks, before, preferred_element_type=jnp.float32
    )
    attended = (inside_block + from_before).reshape(span, heads_here, HEAD)
    gain_rows = lax.dynamic_slice_in_dim(head_gain, core * heads_here, heads_here, 0)
    normed_group = normalize(attended, gain_rows)
    normed_own = pair_exchange(normed_group, core, 0, 1)
    normed_own = normed_own.reshape(tokens_here, H * HEAD)
    columns = gather_finish(parts, sent, jnp.arange(4))
    tokens = jnp.concatenate([normed_own, swap(normed_own, "c")], axis=0)
    wide = jnp.dot(tokens, columns, preferred_element_type=jnp.float32).astype(jnp.bfloat16)
    own_wide = wide[:tokens_here]
    returned = swap(wide[tokens_here:], "c")
    width = own_wide.shape[1] // 2
    by_offset = jnp.stack(
        [
            own_wide[:, :width],
            returned[:, :width],
            own_wide[:, width:],
            returned[:, width:],
        ]
    )
    block = jnp.arange(4)
    offsets = ((block // 2 - half) % 2) * 2 + (block % 2 - core) % 2
    projected = jnp.take(by_offset, offsets, axis=0)
    projected = jnp.transpose(projected, (1, 0, 2)).reshape(tokens_here, -1)
    layer_out = projected[None]
    return (layer_out, updated, moment_one, moment_two)


def solution(mesh):
    fine = Mesh(mesh.devices.reshape(4, 2, 4, 2, 2), DP + SEQ)
    data = P(DP, SEQ, None)
    blocks = P(DP, SEQ)
    in_specs = (data, data, data, P(), blocks, blocks, blocks, blocks)
    out_specs = (data, blocks, blocks, blocks)
    return jax.shard_map(
        on_device, mesh=fine, in_specs=in_specs, out_specs=out_specs, check_vma=False
    )
```

```python
import math

import jax
import jax.numpy as jnp
from jax import lax
from jax.sharding import Mesh, PartitionSpec as P

HEAD = 128
DP = ("z", "xl", "y")
SEQ = ("xh", "c")
H = 20
CH = 128


beta_one = 0.9
beta_two = 0.95
learn_rate = 0.0003
decay_rate = 0.1
adam_eps = 1e-08
step_count = 100
norm_eps = 1e-06


def ring_send(x, axis, size):
    if size == 2:
        return (lax.ppermute(x, axis, [(0, 1), (1, 0)]),)
    forward = [(k, (k + 1) % size) for k in range(size)]
    backward = [(k, (k - 1) % size) for k in range(size)]
    return (lax.ppermute(x, axis, forward), lax.ppermute(x, axis, backward))


def ring_far(received, axis, size):
    if size == 2:
        return received
    forward = [(k, (k + 1) % size) for k in range(size)]
    backward = [(k, (k - 1) % size) for k in range(size)]
    from_left, from_right = received
    half = from_left.shape[0] // 2
    far = jnp.concatenate(
        [
            lax.ppermute(from_left[:half], axis, forward),
            lax.ppermute(from_right[half:], axis, backward),
        ],
        axis=0,
    )
    return (from_left, far, from_right)


def ring_finish(x, received):
    return jnp.stack((x,) + tuple(received))


def ring_gather(x, axis, size):
    return ring_finish(x, ring_far(ring_send(x, axis, size), axis, size))


STAGES = (("y", "z"), ("z", "y"))


def gather_start(weights):
    width = weights.shape[1] // 2
    parts = []
    for number, (first, _) in enumerate(STAGES):
        part = weights[:, width * number : width * (number + 1)]
        part = ring_gather(part, "xl", 2)
        parts.append(ring_gather(part, first, 4))
    return parts


def gather_finish(parts, sent):
    z = lax.axis_index("z")
    xl = lax.axis_index("xl")
    y = lax.axis_index("y")
    stacked = jnp.arange(32)
    pieces = []
    for part, received, (first, _) in zip(parts, sent, STAGES):
        part = ring_finish(part, received)
        outer, inner, xl_rel = stacked // 8, (stacked // 2) % 4, stacked % 2
        z_rel, y_rel = (outer, inner) if first == "y" else (inner, outer)
        source = ((z - z_rel) % 4) * 8 + ((xl - xl_rel) % 2) * 4 + (y - y_rel) % 4
        pieces.append((part.reshape(-1, part.shape[-1]), source))
    return pieces


def seq_shift(x, shift):
    return lax.ppermute(x, SEQ, [(k, (k + shift) % 4) for k in range(4)])

def featurize(block, offset, seq_length):
    positions = (offset + jnp.arange(block.shape[0], dtype=jnp.int32)).astype(jnp.float32)
    angles = positions * (math.pi / (2.0 * seq_length))
    rectified = jnp.maximum(block.astype(jnp.float32), 0.0)
    cosine = rectified * jnp.cos(angles)[:, None, None]
    sine = rectified * jnp.sin(angles)[:, None, None]
    return jnp.concatenate([cosine, sine], axis=2).astype(jnp.bfloat16)


def to_blocks(x):
    return x.reshape((x.shape[0] // CH, CH) + x.shape[1:])


def normalize(attended, gain_rows):
    mean_square = jnp.mean(attended * attended, axis=2, keepdims=True)
    return (attended * lax.rsqrt(mean_square + norm_eps) * gain_rows[None]).astype(jnp.bfloat16)


def swap(x, axis):
    return lax.ppermute(x, axis, [(0, 1), (1, 0)])


def pair_exchange(x, core, keep_axis, join_axis):
    size = x.shape[keep_axis] // 2
    mine = lax.dynamic_slice_in_dim(x, core * size, size, keep_axis)
    theirs = lax.dynamic_slice_in_dim(x, (1 - core) * size, size, keep_axis)
    received = swap(theirs, "c")
    return jnp.where(
        core == 0,
        jnp.concatenate([mine, received], axis=join_axis),
        jnp.concatenate([received, mine], axis=join_axis),
    )


def on_device(
    queries, keys_in, values_in, head_gain, master_weight, gradient, first_moment, second_moment
):
    moment_one = beta_one * first_moment + (1.0 - beta_one) * gradient
    moment_two = beta_two * second_moment + (1.0 - beta_two) * gradient * gradient
    corrected = (
        moment_one
        / (1.0 - beta_one**step_count)
        / (jnp.sqrt(moment_two / (1.0 - beta_two**step_count)) + adam_eps)
    )
    updated = master_weight - learn_rate * (corrected + decay_rate * master_weight)
    weights = updated.astype(jnp.bfloat16)
    tokens_here = queries.shape[1]
    seq_length = tokens_here * lax.axis_size(SEQ)
    half = lax.axis_index("xh")
    core = lax.axis_index("c")
    heads_here = H // 2
    both = jnp.concatenate([weights, swap(weights, "xh")], axis=1)
    parts = gather_start(both)
    parts, query_heads = lax.optimization_barrier(
        (parts, queries[0].reshape(tokens_here, H, HEAD))
    )
    query_group = pair_exchange(query_heads, core, 1, 0)
    sent = [ring_send(part, second, 4) for part, (_, second) in zip(parts, STAGES)]
    sent, key_heads = lax.optimization_barrier((sent, keys_in[0].reshape(tokens_here, H, HEAD)))
    key_group = pair_exchange(key_heads, core, 1, 0)
    sent = [ring_far(received, second, 4) for received, (_, second) in zip(sent, STAGES)]
    sent, value_heads = lax.optimization_barrier(
        (sent, values_in[0].reshape(tokens_here, H, HEAD))
    )
    value_group = pair_exchange(value_heads, core, 1, 0)
    span = query_group.shape[0]
    offset = half * span
    query_blocks = to_blocks(featurize(query_group, offset, seq_length))
    key_blocks = to_blocks(featurize(key_group, offset, seq_length))
    value_blocks = to_blocks(value_group)
    states = jnp.einsum(
        "cjhf,cjhe->chfe", key_blocks, value_blocks, preferred_element_type=jnp.float32
    )
    chip_total = jnp.sum(states, axis=0)
    earlier = lax.ppermute(chip_total, "xh", [(0, 1)])
    scores = jnp.einsum(
        "cihf,cjhf->chij", query_blocks, key_blocks, preferred_element_type=jnp.float32
    )
    causal_mask = jnp.arange(CH)[:, None] >= jnp.arange(CH)[None, :]
    scores = jnp.where(causal_mask[None, None], scores, 0.0).astype(jnp.bfloat16)
    inside_block = jnp.einsum(
        "chij,cjhe->cihe", scores, value_blocks, preferred_element_type=jnp.float32
    )
    running = jnp.cumsum(states, axis=0)
    local_before = jnp.concatenate([jnp.zeros_like(states[:1]), running[:-1]], axis=0)
    before = (earlier[None] + local_before).astype(jnp.bfloat16)
    from_before = jnp.einsum(
        "cihf,chfe->cihe", query_blocks, before, preferred_element_type=jnp.float32
    )
    attended = (inside_block + from_before).reshape(span, heads_here, HEAD)
    gain_rows = lax.dynamic_slice_in_dim(head_gain, core * heads_here, heads_here, 0)
    normed_group = normalize(attended, gain_rows)
    normed_own = pair_exchange(normed_group, core, 0, 1)
    normed_own = normed_own.reshape(tokens_here, H * HEAD)
    tokens = jnp.concatenate([normed_own, swap(normed_own, "c")], axis=0)
    by_block = tokens.reshape(tokens.shape[0], 32, -1)
    wide = []
    for rows, source in gather_finish(parts, sent):
        features = jnp.take(by_block, source, axis=1).reshape(tokens.shape)
        wide.append(
            jnp.dot(features, rows, preferred_element_type=jnp.float32).astype(jnp.bfloat16)
        )
    own = [piece[:tokens_here] for piece in wide]
    returned = [swap(piece[tokens_here:], "c") for piece in wide]
    candidates = own + returned

    def place(chip, side):
        order = []
        for block in range(4):
            from_partner = (block % 2 - side) % 2
            order.append(2 * from_partner + (block // 2 - chip) % 2)
        return lambda *pieces: jnp.concatenate([pieces[i] for i in order], axis=1)

    branches = [place(chip, side) for chip in (0, 1) for side in (0, 1)]
    projected = lax.switch(half * 2 + core, branches, *candidates)
    layer_out = projected[None]
    return (layer_out, updated, moment_one, moment_two)


def solution(mesh):
    fine = Mesh(mesh.devices.reshape(4, 2, 4, 2, 2), DP + SEQ)
    data = P(DP, SEQ, None)
    blocks = P(DP, SEQ)
    in_specs = (data, data, data, P(), blocks, blocks, blocks, blocks)
    out_specs = (data, blocks, blocks, blocks)
    return jax.shard_map(
        on_device, mesh=fine, in_specs=in_specs, out_specs=out_specs, check_vma=False
    )
```

```python
import math

import jax
import jax.numpy as jnp
from jax import lax
from jax.sharding import Mesh, PartitionSpec as P

HEAD = 128
DP = ("z", "xl", "y")
SEQ = ("xh", "c")
H = 20
CH = 128


beta_one = 0.9
beta_two = 0.95
learn_rate = 0.0003
decay_rate = 0.1
adam_eps = 1e-08
step_count = 100
norm_eps = 1e-06


def ring_send(x, axis, size):
    if size == 2:
        return (lax.ppermute(x, axis, [(0, 1), (1, 0)]),)
    forward = [(k, (k + 1) % size) for k in range(size)]
    backward = [(k, (k - 1) % size) for k in range(size)]
    return (lax.ppermute(x, axis, forward), lax.ppermute(x, axis, backward))


def ring_far(received, axis, size):
    if size == 2:
        return received
    forward = [(k, (k + 1) % size) for k in range(size)]
    backward = [(k, (k - 1) % size) for k in range(size)]
    from_left, from_right = received
    half = from_left.shape[0] // 2
    far = jnp.concatenate(
        [
            lax.ppermute(from_left[:half], axis, forward),
            lax.ppermute(from_right[half:], axis, backward),
        ],
        axis=0,
    )
    return (from_left, far, from_right)


def ring_finish(x, received):
    return jnp.stack((x,) + tuple(received))


def ring_gather(x, axis, size):
    return ring_finish(x, ring_far(ring_send(x, axis, size), axis, size))


STAGES = (("y", "z"), ("z", "y"))


def gather_start(weights):
    width = weights.shape[1] // 2
    parts = []
    for number, (first, _) in enumerate(STAGES):
        part = weights[:, width * number : width * (number + 1)]
        part = ring_gather(part, "xl", 2)
        parts.append(ring_gather(part, first, 4))
    return parts


def gather_finish(parts, sent):
    z = lax.axis_index("z")
    xl = lax.axis_index("xl")
    y = lax.axis_index("y")
    stacked = jnp.arange(32)
    pieces = []
    for part, received, (first, _) in zip(parts, sent, STAGES):
        part = ring_finish(part, received)
        outer, inner, xl_rel = stacked // 8, (stacked // 2) % 4, stacked % 2
        z_rel, y_rel = (outer, inner) if first == "y" else (inner, outer)
        source = ((z - z_rel) % 4) * 8 + ((xl - xl_rel) % 2) * 4 + (y - y_rel) % 4
        pieces.append((part.reshape(-1, part.shape[-1]), source))
    return pieces


def seq_shift(x, shift):
    return lax.ppermute(x, SEQ, [(k, (k + shift) % 4) for k in range(4)])

def featurize(block, offset, seq_length):
    positions = (offset + jnp.arange(block.shape[0], dtype=jnp.int32)).astype(jnp.float32)
    angles = positions * (math.pi / (2.0 * seq_length))
    rectified = jnp.maximum(block.astype(jnp.float32), 0.0)
    cosine = rectified * jnp.cos(angles)[:, None, None]
    sine = rectified * jnp.sin(angles)[:, None, None]
    return jnp.concatenate([cosine, sine], axis=2).astype(jnp.bfloat16)


def to_blocks(x):
    return x.reshape((x.shape[0] // CH, CH) + x.shape[1:])


def normalize(attended, gain_rows):
    mean_square = jnp.mean(attended * attended, axis=2, keepdims=True)
    return (attended * lax.rsqrt(mean_square + norm_eps) * gain_rows[None]).astype(jnp.bfloat16)


def swap(x, axis):
    return lax.ppermute(x, axis, [(0, 1), (1, 0)])


def pair_exchange(x, core, keep_axis, join_axis):
    size = x.shape[keep_axis] // 2
    mine = lax.dynamic_slice_in_dim(x, core * size, size, keep_axis)
    theirs = lax.dynamic_slice_in_dim(x, (1 - core) * size, size, keep_axis)
    received = swap(theirs, "c")
    return jnp.where(
        core == 0,
        jnp.concatenate([mine, received], axis=join_axis),
        jnp.concatenate([received, mine], axis=join_axis),
    )


def on_device(
    queries, keys_in, values_in, head_gain, master_weight, gradient, first_moment, second_moment
):
    moment_one = beta_one * first_moment + (1.0 - beta_one) * gradient
    moment_two = beta_two * second_moment + (1.0 - beta_two) * gradient * gradient
    corrected = (
        moment_one
        / (1.0 - beta_one**step_count)
        / (jnp.sqrt(moment_two / (1.0 - beta_two**step_count)) + adam_eps)
    )
    updated = master_weight - learn_rate * (corrected + decay_rate * master_weight)
    weights = updated.astype(jnp.bfloat16)
    tokens_here = queries.shape[1]
    seq_length = tokens_here * lax.axis_size(SEQ)
    half = lax.axis_index("xh")
    core = lax.axis_index("c")
    heads_here = H // 2
    both = jnp.concatenate([weights, swap(weights, "xh")], axis=1)
    parts = gather_start(both)
    parts, query_heads = lax.optimization_barrier(
        (parts, queries[0].reshape(tokens_here, H, HEAD))
    )
    query_group = pair_exchange(query_heads, core, 1, 0)
    sent = [ring_send(part, second, 4) for part, (_, second) in zip(parts, STAGES)]
    key_group = pair_exchange(keys_in[0].reshape(tokens_here, H, HEAD), core, 1, 0)
    value_group = pair_exchange(values_in[0].reshape(tokens_here, H, HEAD), core, 1, 0)
    span = query_group.shape[0]
    offset = half * span
    query_blocks = to_blocks(featurize(query_group, offset, seq_length))
    key_blocks = to_blocks(featurize(key_group, offset, seq_length))
    value_blocks = to_blocks(value_group)
    states = jnp.einsum(
        "cjhf,cjhe->chfe", key_blocks, value_blocks, preferred_element_type=jnp.float32
    )
    chip_total = jnp.sum(states, axis=0)
    sent, chip_total = lax.optimization_barrier((sent, chip_total))
    sent = [ring_far(received, second, 4) for received, (_, second) in zip(sent, STAGES)]
    earlier = lax.ppermute(chip_total, "xh", [(0, 1)])
    scores = jnp.einsum(
        "cihf,cjhf->chij", query_blocks, key_blocks, preferred_element_type=jnp.float32
    )
    causal_mask = jnp.arange(CH)[:, None] >= jnp.arange(CH)[None, :]
    scores = jnp.where(causal_mask[None, None], scores, 0.0).astype(jnp.bfloat16)
    inside_block = jnp.einsum(
        "chij,cjhe->cihe", scores, value_blocks, preferred_element_type=jnp.float32
    )
    running = jnp.cumsum(states, axis=0)
    local_before = jnp.concatenate([jnp.zeros_like(states[:1]), running[:-1]], axis=0)
    before = (earlier[None] + local_before).astype(jnp.bfloat16)
    from_before = jnp.einsum(
        "cihf,chfe->cihe", query_blocks, before, preferred_element_type=jnp.float32
    )
    attended = (inside_block + from_before).reshape(span, heads_here, HEAD)
    sent, attended = lax.optimization_barrier((sent, attended))
    gain_rows = lax.dynamic_slice_in_dim(head_gain, core * heads_here, heads_here, 0)
    normed_group = normalize(attended, gain_rows)
    normed_own = pair_exchange(normed_group, core, 0, 1)
    normed_own = normed_own.reshape(tokens_here, H * HEAD)
    tokens = jnp.concatenate([normed_own, swap(normed_own, "c")], axis=0)
    by_block = tokens.reshape(tokens.shape[0], 32, -1)
    wide = []
    for rows, source in gather_finish(parts, sent):
        features = jnp.take(by_block, source, axis=1).reshape(tokens.shape)
        wide.append(
            jnp.dot(features, rows, preferred_element_type=jnp.float32).astype(jnp.bfloat16)
        )
    own = [piece[:tokens_here] for piece in wide]
    returned = [swap(piece[tokens_here:], "c") for piece in wide]
    candidates = own + returned

    def place(chip, side):
        order = []
        for block in range(4):
            from_partner = (block % 2 - side) % 2
            order.append(2 * from_partner + (block // 2 - chip) % 2)
        return lambda *pieces: jnp.concatenate([pieces[i] for i in order], axis=1)

    branches = [place(chip, side) for chip in (0, 1) for side in (0, 1)]
    projected = lax.switch(half * 2 + core, branches, *candidates)
    layer_out = projected[None]
    return (layer_out, updated, moment_one, moment_two)


def solution(mesh):
    fine = Mesh(mesh.devices.reshape(4, 2, 4, 2, 2), DP + SEQ)
    data = P(DP, SEQ, None)
    blocks = P(DP, SEQ)
    in_specs = (data, data, data, P(), blocks, blocks, blocks, blocks)
    out_specs = (data, blocks, blocks, blocks)
    return jax.shard_map(
        on_device, mesh=fine, in_specs=in_specs, out_specs=out_specs, check_vma=False
    )
```

```python
import math

import jax
import jax.numpy as jnp
from jax import lax
from jax.sharding import Mesh, PartitionSpec as P

HEAD = 128
DP = ("z", "xl", "y")
SEQ = ("xh", "c")
H = 20
CH = 128


beta_one = 0.9
beta_two = 0.95
learn_rate = 0.0003
decay_rate = 0.1
adam_eps = 1e-08
step_count = 100
norm_eps = 1e-06


def ring_send(x, axis, size):
    if size == 2:
        return (lax.ppermute(x, axis, [(0, 1), (1, 0)]),)
    forward = [(k, (k + 1) % size) for k in range(size)]
    backward = [(k, (k - 1) % size) for k in range(size)]
    return (lax.ppermute(x, axis, forward), lax.ppermute(x, axis, backward))


def ring_far(received, axis, size):
    if size == 2:
        return received
    forward = [(k, (k + 1) % size) for k in range(size)]
    backward = [(k, (k - 1) % size) for k in range(size)]
    from_left, from_right = received
    half = from_left.shape[0] // 2
    far = jnp.concatenate(
        [
            lax.ppermute(from_left[:half], axis, forward),
            lax.ppermute(from_right[half:], axis, backward),
        ],
        axis=0,
    )
    return (from_left, far, from_right)


def ring_finish(x, received):
    return jnp.stack((x,) + tuple(received))


def ring_gather(x, axis, size):
    return ring_finish(x, ring_far(ring_send(x, axis, size), axis, size))


STAGES = (("y", "z"), ("z", "y"))


def ring_direct(x, axis, size):
    shifted = [
        lax.ppermute(x, axis, [(k, (k + shift) % size) for k in range(size)])
        for shift in (1, 2, 3)
    ]
    return jnp.stack([x] + shifted)


def gather_start(weights):
    near = swap(weights, "xl")
    peer = swap(weights, "xh")
    diagonal = lax.ppermute(weights, ("xl", "xh"), [(k, 3 - k) for k in range(4)])
    halves = (jnp.stack([weights, near]), jnp.stack([peer, diagonal]))
    return [ring_direct(part, first, 4) for part, (first, _) in zip(halves, STAGES)]


def gather_finish(parts, sent):
    z = lax.axis_index("z")
    xl = lax.axis_index("xl")
    y = lax.axis_index("y")
    stacked = jnp.arange(32)
    pieces = []
    for part, received, (first, _) in zip(parts, sent, STAGES):
        part = ring_finish(part, received)
        outer, inner, xl_rel = stacked // 8, (stacked // 2) % 4, stacked % 2
        z_rel, y_rel = (outer, inner) if first == "y" else (inner, outer)
        source = ((z - z_rel) % 4) * 8 + ((xl - xl_rel) % 2) * 4 + (y - y_rel) % 4
        pieces.append((part.reshape(-1, part.shape[-1]), source))
    return pieces


def seq_shift(x, shift):
    return lax.ppermute(x, SEQ, [(k, (k + shift) % 4) for k in range(4)])

def featurize(block, offset, seq_length):
    positions = (offset + jnp.arange(block.shape[0], dtype=jnp.int32)).astype(jnp.float32)
    angles = positions * (math.pi / (2.0 * seq_length))
    rectified = jnp.maximum(block.astype(jnp.float32), 0.0)
    cosine = rectified * jnp.cos(angles)[:, None, None]
    sine = rectified * jnp.sin(angles)[:, None, None]
    return jnp.concatenate([cosine, sine], axis=2).astype(jnp.bfloat16)


def to_blocks(x):
    return x.reshape((x.shape[0] // CH, CH) + x.shape[1:])


def normalize(attended, gain_rows):
    mean_square = jnp.mean(attended * attended, axis=2, keepdims=True)
    return (attended * lax.rsqrt(mean_square + norm_eps) * gain_rows[None]).astype(jnp.bfloat16)


def swap(x, axis):
    return lax.ppermute(x, axis, [(0, 1), (1, 0)])


def pair_exchange(x, core, keep_axis, join_axis):
    size = x.shape[keep_axis] // 2
    mine = lax.dynamic_slice_in_dim(x, core * size, size, keep_axis)
    theirs = lax.dynamic_slice_in_dim(x, (1 - core) * size, size, keep_axis)
    received = swap(theirs, "c")
    return jnp.where(
        core == 0,
        jnp.concatenate([mine, received], axis=join_axis),
        jnp.concatenate([received, mine], axis=join_axis),
    )


def on_device(
    queries, keys_in, values_in, head_gain, master_weight, gradient, first_moment, second_moment
):
    moment_one = beta_one * first_moment + (1.0 - beta_one) * gradient
    moment_two = beta_two * second_moment + (1.0 - beta_two) * gradient * gradient
    corrected = (
        moment_one
        / (1.0 - beta_one**step_count)
        / (jnp.sqrt(moment_two / (1.0 - beta_two**step_count)) + adam_eps)
    )
    updated = master_weight - learn_rate * (corrected + decay_rate * master_weight)
    weights = updated.astype(jnp.bfloat16)
    tokens_here = queries.shape[1]
    seq_length = tokens_here * lax.axis_size(SEQ)
    half = lax.axis_index("xh")
    core = lax.axis_index("c")
    heads_here = H // 2
    parts = gather_start(weights)
    parts, query_heads = lax.optimization_barrier(
        (parts, queries[0].reshape(tokens_here, H, HEAD))
    )
    query_group = pair_exchange(query_heads, core, 1, 0)
    sent = [ring_send(part, second, 4) for part, (_, second) in zip(parts, STAGES)]
    key_group = pair_exchange(keys_in[0].reshape(tokens_here, H, HEAD), core, 1, 0)
    value_group = pair_exchange(values_in[0].reshape(tokens_here, H, HEAD), core, 1, 0)
    span = query_group.shape[0]
    offset = half * span
    query_blocks = to_blocks(featurize(query_group, offset, seq_length))
    key_blocks = to_blocks(featurize(key_group, offset, seq_length))
    value_blocks = to_blocks(value_group)
    states = jnp.einsum(
        "cjhf,cjhe->chfe", key_blocks, value_blocks, preferred_element_type=jnp.float32
    )
    chip_total = jnp.sum(states, axis=0)
    sent, chip_total = lax.optimization_barrier((sent, chip_total))
    sent = [ring_far(received, second, 4) for received, (_, second) in zip(sent, STAGES)]
    earlier = lax.ppermute(chip_total, "xh", [(0, 1)])
    scores = jnp.einsum(
        "cihf,cjhf->chij", query_blocks, key_blocks, preferred_element_type=jnp.float32
    )
    causal_mask = jnp.arange(CH)[:, None] >= jnp.arange(CH)[None, :]
    scores = jnp.where(causal_mask[None, None], scores, 0.0).astype(jnp.bfloat16)
    inside_block = jnp.einsum(
        "chij,cjhe->cihe", scores, value_blocks, preferred_element_type=jnp.float32
    )
    running = jnp.cumsum(states, axis=0)
    local_before = jnp.concatenate([jnp.zeros_like(states[:1]), running[:-1]], axis=0)
    before = (earlier[None] + local_before).astype(jnp.bfloat16)
    from_before = jnp.einsum(
        "cihf,chfe->cihe", query_blocks, before, preferred_element_type=jnp.float32
    )
    attended = (inside_block + from_before).reshape(span, heads_here, HEAD)
    sent, attended = lax.optimization_barrier((sent, attended))
    gain_rows = lax.dynamic_slice_in_dim(head_gain, core * heads_here, heads_here, 0)
    normed_group = normalize(attended, gain_rows)
    normed_own = pair_exchange(normed_group, core, 0, 1)
    normed_own = normed_own.reshape(tokens_here, H * HEAD)
    tokens = jnp.concatenate([normed_own, swap(normed_own, "c")], axis=0)
    by_block = tokens.reshape(tokens.shape[0], 32, -1)
    wide = []
    for rows, source in gather_finish(parts, sent):
        features = jnp.take(by_block, source, axis=1).reshape(tokens.shape)
        wide.append(
            jnp.dot(features, rows, preferred_element_type=jnp.float32).astype(jnp.bfloat16)
        )
    own = [piece[:tokens_here] for piece in wide]
    returned = [swap(piece[tokens_here:], "c") for piece in wide]
    candidates = own + returned

    def place(chip, side):
        order = []
        for block in range(4):
            from_partner = (block % 2 - side) % 2
            order.append(2 * from_partner + (block // 2 - chip) % 2)
        return lambda *pieces: jnp.concatenate([pieces[i] for i in order], axis=1)

    branches = [place(chip, side) for chip in (0, 1) for side in (0, 1)]
    projected = lax.switch(half * 2 + core, branches, *candidates)
    layer_out = projected[None]
    return (layer_out, updated, moment_one, moment_two)


def solution(mesh):
    fine = Mesh(mesh.devices.reshape(4, 2, 4, 2, 2), DP + SEQ)
    data = P(DP, SEQ, None)
    blocks = P(DP, SEQ)
    in_specs = (data, data, data, P(), blocks, blocks, blocks, blocks)
    out_specs = (data, blocks, blocks, blocks)
    return jax.shard_map(
        on_device, mesh=fine, in_specs=in_specs, out_specs=out_specs, check_vma=False
    )
```

```python
import math

import jax
import jax.numpy as jnp
from jax import lax
from jax.sharding import Mesh, PartitionSpec as P

HEAD = 128
DP = ("z", "xl", "y")
SEQ = ("xh", "c")
H = 20
CH = 128


beta_one = 0.9
beta_two = 0.95
learn_rate = 0.0003
decay_rate = 0.1
adam_eps = 1e-08
step_count = 100
norm_eps = 1e-06


def ring_send(x, axis, size):
    if size == 2:
        return (lax.ppermute(x, axis, [(0, 1), (1, 0)]),)
    forward = [(k, (k + 1) % size) for k in range(size)]
    backward = [(k, (k - 1) % size) for k in range(size)]
    return (lax.ppermute(x, axis, forward), lax.ppermute(x, axis, backward))


def ring_far(received, axis, size):
    if size == 2:
        return received
    forward = [(k, (k + 1) % size) for k in range(size)]
    backward = [(k, (k - 1) % size) for k in range(size)]
    from_left, from_right = received
    half = from_left.shape[0] // 2
    far = jnp.concatenate(
        [
            lax.ppermute(from_left[:half], axis, forward),
            lax.ppermute(from_right[half:], axis, backward),
        ],
        axis=0,
    )
    return (from_left, far, from_right)


def ring_finish(x, received):
    return jnp.stack((x,) + tuple(received))


def ring_gather(x, axis, size):
    return ring_finish(x, ring_far(ring_send(x, axis, size), axis, size))


STAGES = (("y", "z"), ("z", "y"))


def ring_direct(x, axis, size):
    shifted = [
        lax.ppermute(x, axis, [(k, (k + shift) % size) for k in range(size)])
        for shift in (1, 2, 3)
    ]
    return jnp.stack([x] + shifted)


def gather_start(weights):
    near = swap(weights, "xl")
    peer = swap(weights, "xh")
    diagonal = lax.ppermute(weights, ("xl", "xh"), [(k, 3 - k) for k in range(4)])
    halves = (jnp.stack([weights, near]), jnp.stack([peer, diagonal]))
    return [ring_direct(part, first, 4) for part, (first, _) in zip(halves, STAGES)]


def gather_finish(parts, sent):
    z = lax.axis_index("z")
    xl = lax.axis_index("xl")
    y = lax.axis_index("y")
    stacked = jnp.arange(32)
    pieces = []
    for part, received, (first, _) in zip(parts, sent, STAGES):
        part = ring_finish(part, received)
        outer, inner, xl_rel = stacked // 8, (stacked // 2) % 4, stacked % 2
        z_rel, y_rel = (outer, inner) if first == "y" else (inner, outer)
        source = ((z - z_rel) % 4) * 8 + ((xl - xl_rel) % 2) * 4 + (y - y_rel) % 4
        pieces.append((part.reshape(-1, part.shape[-1]), source))
    return pieces


def seq_shift(x, shift):
    return lax.ppermute(x, SEQ, [(k, (k + shift) % 4) for k in range(4)])

def featurize(block, offset, seq_length):
    positions = (offset + jnp.arange(block.shape[0], dtype=jnp.int32)).astype(jnp.float32)
    angles = positions * (math.pi / (2.0 * seq_length))
    rectified = jnp.maximum(block.astype(jnp.float32), 0.0)
    cosine = rectified * jnp.cos(angles)[:, None, None]
    sine = rectified * jnp.sin(angles)[:, None, None]
    return jnp.concatenate([cosine, sine], axis=2).astype(jnp.bfloat16)


def to_blocks(x):
    return x.reshape((x.shape[0] // CH, CH) + x.shape[1:])


def normalize(attended, gain_rows):
    mean_square = jnp.mean(attended * attended, axis=2, keepdims=True)
    return (attended * lax.rsqrt(mean_square + norm_eps) * gain_rows[None]).astype(jnp.bfloat16)


def swap(x, axis):
    return lax.ppermute(x, axis, [(0, 1), (1, 0)])


def pair_exchange(x, core, keep_axis, join_axis):
    size = x.shape[keep_axis] // 2
    mine = lax.dynamic_slice_in_dim(x, core * size, size, keep_axis)
    theirs = lax.dynamic_slice_in_dim(x, (1 - core) * size, size, keep_axis)
    received = swap(theirs, "c")
    return jnp.where(
        core == 0,
        jnp.concatenate([mine, received], axis=join_axis),
        jnp.concatenate([received, mine], axis=join_axis),
    )


def on_device(
    queries, keys_in, values_in, head_gain, master_weight, gradient, first_moment, second_moment
):
    moment_one = beta_one * first_moment + (1.0 - beta_one) * gradient
    moment_two = beta_two * second_moment + (1.0 - beta_two) * gradient * gradient
    corrected = (
        moment_one
        / (1.0 - beta_one**step_count)
        / (jnp.sqrt(moment_two / (1.0 - beta_two**step_count)) + adam_eps)
    )
    updated = master_weight - learn_rate * (corrected + decay_rate * master_weight)
    weights = updated.astype(jnp.bfloat16)
    tokens_here = queries.shape[1]
    seq_length = tokens_here * lax.axis_size(SEQ)
    half = lax.axis_index("xh")
    core = lax.axis_index("c")
    heads_here = H // 2
    parts = gather_start(weights)
    parts, query_heads = lax.optimization_barrier(
        (parts, queries[0].reshape(tokens_here, H, HEAD))
    )
    local_offset = (half * 2 + core) * tokens_here
    query_group = pair_exchange(featurize(query_heads, local_offset, seq_length), core, 1, 0)
    sent = [ring_send(part, second, 4) for part, (_, second) in zip(parts, STAGES)]
    key_heads = keys_in[0].reshape(tokens_here, H, HEAD)
    key_group = pair_exchange(featurize(key_heads, local_offset, seq_length), core, 1, 0)
    value_group = pair_exchange(values_in[0].reshape(tokens_here, H, HEAD), core, 1, 0)
    span = query_group.shape[0]
    query_blocks = to_blocks(query_group)
    key_blocks = to_blocks(key_group)
    value_blocks = to_blocks(value_group)
    states = jnp.einsum(
        "cjhf,cjhe->chfe", key_blocks, value_blocks, preferred_element_type=jnp.float32
    )
    chip_total = jnp.sum(states, axis=0)
    sent, chip_total = lax.optimization_barrier((sent, chip_total))
    sent = [ring_far(received, second, 4) for received, (_, second) in zip(sent, STAGES)]
    earlier = lax.ppermute(chip_total, "xh", [(0, 1)])
    scores = jnp.einsum(
        "cihf,cjhf->chij", query_blocks, key_blocks, preferred_element_type=jnp.float32
    )
    causal_mask = jnp.arange(CH)[:, None] >= jnp.arange(CH)[None, :]
    scores = jnp.where(causal_mask[None, None], scores, 0.0).astype(jnp.bfloat16)
    inside_block = jnp.einsum(
        "chij,cjhe->cihe", scores, value_blocks, preferred_element_type=jnp.float32
    )
    running = jnp.cumsum(states, axis=0)
    local_before = jnp.concatenate([jnp.zeros_like(states[:1]), running[:-1]], axis=0)
    before = (earlier[None] + local_before).astype(jnp.bfloat16)
    from_before = jnp.einsum(
        "cihf,chfe->cihe", query_blocks, before, preferred_element_type=jnp.float32
    )
    attended = (inside_block + from_before).reshape(span, heads_here, HEAD)
    sent, attended = lax.optimization_barrier((sent, attended))
    gain_rows = lax.dynamic_slice_in_dim(head_gain, core * heads_here, heads_here, 0)
    normed_group = normalize(attended, gain_rows)
    normed_own = pair_exchange(normed_group, core, 0, 1)
    normed_own = normed_own.reshape(tokens_here, H * HEAD)
    tokens = jnp.concatenate([normed_own, swap(normed_own, "c")], axis=0)
    by_block = tokens.reshape(tokens.shape[0], 32, -1)
    wide = []
    for rows, source in gather_finish(parts, sent):
        features = jnp.take(by_block, source, axis=1, mode="clip").reshape(tokens.shape)
        wide.append(
            jnp.dot(features, rows, preferred_element_type=jnp.float32).astype(jnp.bfloat16)
        )
    own = [piece[:tokens_here] for piece in wide]
    returned = [swap(piece[tokens_here:], "c") for piece in wide]
    candidates = own + returned

    def place(chip, side):
        order = []
        for block in range(4):
            from_partner = (block % 2 - side) % 2
            order.append(2 * from_partner + (block // 2 - chip) % 2)
        return lambda *pieces: jnp.concatenate([pieces[i] for i in order], axis=1)

    branches = [place(chip, side) for chip in (0, 1) for side in (0, 1)]
    projected = lax.switch(half * 2 + core, branches, *candidates)
    layer_out = projected[None]
    return (layer_out, updated, moment_one, moment_two)


def solution(mesh):
    fine = Mesh(mesh.devices.reshape(4, 2, 4, 2, 2), DP + SEQ)
    data = P(DP, SEQ, None)
    blocks = P(DP, SEQ)
    in_specs = (data, data, data, P(), blocks, blocks, blocks, blocks)
    out_specs = (data, blocks, blocks, blocks)
    return jax.shard_map(
        on_device, mesh=fine, in_specs=in_specs, out_specs=out_specs, check_vma=False
    )
```

```python
import math

import jax
import jax.numpy as jnp
from jax import lax
from jax.sharding import Mesh, PartitionSpec as P

HEAD = 128
DP = ("z", "xl", "y")
SEQ = ("xh", "c")
H = 20
CH = 128


beta_one = 0.9
beta_two = 0.95
learn_rate = 0.0003
decay_rate = 0.1
adam_eps = 1e-08
step_count = 100
norm_eps = 1e-06


def ring_send(x, axis, size):
    if size == 2:
        return (lax.ppermute(x, axis, [(0, 1), (1, 0)]),)
    forward = [(k, (k + 1) % size) for k in range(size)]
    backward = [(k, (k - 1) % size) for k in range(size)]
    return (lax.ppermute(x, axis, forward), lax.ppermute(x, axis, backward))


def ring_far(received, axis, size):
    if size == 2:
        return received
    forward = [(k, (k + 1) % size) for k in range(size)]
    backward = [(k, (k - 1) % size) for k in range(size)]
    from_left, from_right = received
    half = from_left.shape[0] // 2
    far = jnp.concatenate(
        [
            lax.ppermute(from_left[:half], axis, forward),
            lax.ppermute(from_right[half:], axis, backward),
        ],
        axis=0,
    )
    return (from_left, far, from_right)


def ring_finish(x, received):
    return jnp.stack((x,) + tuple(received))


def ring_gather(x, axis, size):
    return ring_finish(x, ring_far(ring_send(x, axis, size), axis, size))


STAGES = (("y", "z"), ("z", "y"))


def ring_direct(x, axis, size):
    shifted = [
        lax.ppermute(x, axis, [(k, (k + shift) % size) for k in range(size)])
        for shift in (1, 2, 3)
    ]
    return jnp.stack([x] + shifted)


def gather_start(weights):
    near = swap(weights, "xl")
    peer = swap(weights, "xh")
    diagonal = lax.ppermute(weights, ("xl", "xh"), [(k, 3 - k) for k in range(4)])
    halves = (jnp.stack([weights, near]), jnp.stack([peer, diagonal]))
    return [ring_direct(part, first, 4) for part, (first, _) in zip(halves, STAGES)]


def gather_finish(parts, sent):
    z = lax.axis_index("z")
    xl = lax.axis_index("xl")
    y = lax.axis_index("y")
    stacked = jnp.arange(32)
    pieces = []
    for part, received, (first, _) in zip(parts, sent, STAGES):
        part = ring_finish(part, received)
        outer, inner, xl_rel = stacked // 8, (stacked // 2) % 4, stacked % 2
        z_rel, y_rel = (outer, inner) if first == "y" else (inner, outer)
        source = ((z - z_rel) % 4) * 8 + ((xl - xl_rel) % 2) * 4 + (y - y_rel) % 4
        pieces.append((part.reshape(-1, part.shape[-1]), source))
    return pieces


def seq_shift(x, shift):
    return lax.ppermute(x, SEQ, [(k, (k + shift) % 4) for k in range(4)])

def featurize(block, offset, seq_length):
    positions = (offset + jnp.arange(block.shape[0], dtype=jnp.int32)).astype(jnp.float32)
    angles = positions * (math.pi / (2.0 * seq_length))
    rectified = jnp.maximum(block.astype(jnp.float32), 0.0)
    cosine = rectified * jnp.cos(angles)[:, None, None]
    sine = rectified * jnp.sin(angles)[:, None, None]
    return jnp.concatenate([cosine, sine], axis=2).astype(jnp.bfloat16)


def to_blocks(x):
    return x.reshape((x.shape[0] // CH, CH) + x.shape[1:])


def normalize(attended, gain_rows):
    mean_square = jnp.mean(attended * attended, axis=2, keepdims=True)
    return (attended * lax.rsqrt(mean_square + norm_eps) * gain_rows[None]).astype(jnp.bfloat16)


def swap(x, axis):
    return lax.ppermute(x, axis, [(0, 1), (1, 0)])


def pair_exchange(x, core, keep_axis, join_axis):
    size = x.shape[keep_axis] // 2
    mine = lax.dynamic_slice_in_dim(x, core * size, size, keep_axis)
    theirs = lax.dynamic_slice_in_dim(x, (1 - core) * size, size, keep_axis)
    received = swap(theirs, "c")
    return jnp.where(
        core == 0,
        jnp.concatenate([mine, received], axis=join_axis),
        jnp.concatenate([received, mine], axis=join_axis),
    )


def on_device(
    queries, keys_in, values_in, head_gain, master_weight, gradient, first_moment, second_moment
):
    moment_one = beta_one * first_moment + (1.0 - beta_one) * gradient
    moment_two = beta_two * second_moment + (1.0 - beta_two) * gradient * gradient
    corrected = (
        moment_one
        / (1.0 - beta_one**step_count)
        / (jnp.sqrt(moment_two / (1.0 - beta_two**step_count)) + adam_eps)
    )
    updated = master_weight - learn_rate * (corrected + decay_rate * master_weight)
    weights = updated.astype(jnp.bfloat16)
    tokens_here = queries.shape[1]
    seq_length = tokens_here * lax.axis_size(SEQ)
    half = lax.axis_index("xh")
    core = lax.axis_index("c")
    heads_here = H // 2
    parts = gather_start(weights)
    parts, query_heads = lax.optimization_barrier(
        (parts, queries[0].reshape(tokens_here, H, HEAD))
    )
    query_group = pair_exchange(query_heads, core, 1, 0)
    sent = [ring_send(part, second, 4) for part, (_, second) in zip(parts, STAGES)]
    key_value = jnp.stack([keys_in[0], values_in[0]]).reshape(2, tokens_here, H, HEAD)
    key_group, value_group = pair_exchange(key_value, core, 2, 1)
    span = query_group.shape[0]
    offset = half * span
    query_blocks = to_blocks(featurize(query_group, offset, seq_length))
    key_blocks = to_blocks(featurize(key_group, offset, seq_length))
    value_blocks = to_blocks(value_group)
    states = jnp.einsum(
        "cjhf,cjhe->chfe", key_blocks, value_blocks, preferred_element_type=jnp.float32
    )
    chip_total = jnp.sum(states, axis=0)
    sent, chip_total = lax.optimization_barrier((sent, chip_total))
    sent = [ring_far(received, second, 4) for received, (_, second) in zip(sent, STAGES)]
    earlier = lax.ppermute(chip_total, "xh", [(0, 1)])
    scores = jnp.einsum(
        "cihf,cjhf->chij", query_blocks, key_blocks, preferred_element_type=jnp.float32
    )
    causal_mask = jnp.arange(CH)[:, None] >= jnp.arange(CH)[None, :]
    scores = jnp.where(causal_mask[None, None], scores, 0.0).astype(jnp.bfloat16)
    inside_block = jnp.einsum(
        "chij,cjhe->cihe", scores, value_blocks, preferred_element_type=jnp.float32
    )
    running = jnp.cumsum(states, axis=0)
    local_before = jnp.concatenate([jnp.zeros_like(states[:1]), running[:-1]], axis=0)
    before = (earlier[None] + local_before).astype(jnp.bfloat16)
    from_before = jnp.einsum(
        "cihf,chfe->cihe", query_blocks, before, preferred_element_type=jnp.float32
    )
    attended = (inside_block + from_before).reshape(span, heads_here, HEAD)
    sent, attended = lax.optimization_barrier((sent, attended))
    gain_rows = lax.dynamic_slice_in_dim(head_gain, core * heads_here, heads_here, 0)
    normed_group = normalize(attended, gain_rows)
    normed_own = pair_exchange(normed_group, core, 0, 1)
    normed_own = normed_own.reshape(tokens_here, H * HEAD)
    tokens = jnp.concatenate([normed_own, swap(normed_own, "c")], axis=0)
    by_block = tokens.reshape(tokens.shape[0], 32, -1)
    wide = []
    for rows, source in gather_finish(parts, sent):
        features = jnp.take(by_block, source, axis=1, mode="clip").reshape(tokens.shape)
        wide.append(
            jnp.dot(features, rows, preferred_element_type=jnp.float32).astype(jnp.bfloat16)
        )
    own = [piece[:tokens_here] for piece in wide]
    returned = swap(jnp.stack([piece[tokens_here:] for piece in wide]), "c")
    returned = [returned[0], returned[1]]
    candidates = own + returned

    def place(chip, side):
        order = []
        for block in range(4):
            from_partner = (block % 2 - side) % 2
            order.append(2 * from_partner + (block // 2 - chip) % 2)
        return lambda *pieces: jnp.concatenate([pieces[i] for i in order], axis=1)

    branches = [place(chip, side) for chip in (0, 1) for side in (0, 1)]
    projected = lax.switch(half * 2 + core, branches, *candidates)
    layer_out = projected[None]
    return (layer_out, updated, moment_one, moment_two)


def solution(mesh):
    fine = Mesh(mesh.devices.reshape(4, 2, 4, 2, 2), DP + SEQ)
    data = P(DP, SEQ, None)
    blocks = P(DP, SEQ)
    in_specs = (data, data, data, P(), blocks, blocks, blocks, blocks)
    out_specs = (data, blocks, blocks, blocks)
    return jax.shard_map(
        on_device, mesh=fine, in_specs=in_specs, out_specs=out_specs, check_vma=False
    )
```

```python
import math

import jax
import jax.numpy as jnp
from jax import lax
from jax.sharding import Mesh, PartitionSpec as P

HEAD = 128
DP = ("z", "xl", "y")
SEQ = ("xh", "c")
H = 20
CH = 128


beta_one = 0.9
beta_two = 0.95
learn_rate = 0.0003
decay_rate = 0.1
adam_eps = 1e-08
step_count = 100
norm_eps = 1e-06


def ring_send(x, axis, size):
    if size == 2:
        return (lax.ppermute(x, axis, [(0, 1), (1, 0)]),)
    forward = [(k, (k + 1) % size) for k in range(size)]
    backward = [(k, (k - 1) % size) for k in range(size)]
    return (lax.ppermute(x, axis, forward), lax.ppermute(x, axis, backward))


def ring_far(received, axis, size):
    if size == 2:
        return received
    forward = [(k, (k + 1) % size) for k in range(size)]
    backward = [(k, (k - 1) % size) for k in range(size)]
    from_left, from_right = received
    half = from_left.shape[0] // 2
    far = jnp.concatenate(
        [
            lax.ppermute(from_left[:half], axis, forward),
            lax.ppermute(from_right[half:], axis, backward),
        ],
        axis=0,
    )
    return (from_left, far, from_right)


def ring_finish(x, received):
    return jnp.stack((x,) + tuple(received))


def ring_gather(x, axis, size):
    return ring_finish(x, ring_far(ring_send(x, axis, size), axis, size))


STAGES = (("y", "z"), ("z", "y"))


def ring_direct(x, axis, size):
    shifted = [
        lax.ppermute(x, axis, [(k, (k + shift) % size) for k in range(size)])
        for shift in (1, 2, 3)
    ]
    return jnp.stack([x] + shifted)


def gather_first(weights):
    near = swap(weights, "xl")
    peer = swap(weights, "xh")
    diagonal = lax.ppermute(weights, ("xl", "xh"), [(k, 3 - k) for k in range(4)])
    return (jnp.stack([weights, near]), jnp.stack([peer, diagonal]))


def gather_start(halves):
    return [ring_direct(part, first, 4) for part, (first, _) in zip(halves, STAGES)]


def gather_finish(parts, sent):
    z = lax.axis_index("z")
    xl = lax.axis_index("xl")
    y = lax.axis_index("y")
    stacked = jnp.arange(32)
    pieces = []
    for part, received, (first, _) in zip(parts, sent, STAGES):
        part = ring_finish(part, received)
        outer, inner, xl_rel = stacked // 8, (stacked // 2) % 4, stacked % 2
        z_rel, y_rel = (outer, inner) if first == "y" else (inner, outer)
        source = ((z - z_rel) % 4) * 8 + ((xl - xl_rel) % 2) * 4 + (y - y_rel) % 4
        pieces.append((part.reshape(-1, part.shape[-1]), source))
    return pieces


def seq_shift(x, shift):
    return lax.ppermute(x, SEQ, [(k, (k + shift) % 4) for k in range(4)])

def featurize(block, offset, seq_length):
    positions = (offset + jnp.arange(block.shape[0], dtype=jnp.int32)).astype(jnp.float32)
    angles = positions * (math.pi / (2.0 * seq_length))
    rectified = jnp.maximum(block.astype(jnp.float32), 0.0)
    cosine = rectified * jnp.cos(angles)[:, None, None]
    sine = rectified * jnp.sin(angles)[:, None, None]
    return jnp.concatenate([cosine, sine], axis=2).astype(jnp.bfloat16)


def to_blocks(x):
    return x.reshape((x.shape[0] // CH, CH) + x.shape[1:])


def normalize(attended, gain_rows):
    mean_square = jnp.mean(attended * attended, axis=2, keepdims=True)
    return (attended * lax.rsqrt(mean_square + norm_eps) * gain_rows[None]).astype(jnp.bfloat16)


def swap(x, axis):
    return lax.ppermute(x, axis, [(0, 1), (1, 0)])


def pair_exchange(x, core, keep_axis, join_axis):
    size = x.shape[keep_axis] // 2
    mine = lax.dynamic_slice_in_dim(x, core * size, size, keep_axis)
    theirs = lax.dynamic_slice_in_dim(x, (1 - core) * size, size, keep_axis)
    received = swap(theirs, "c")
    return jnp.where(
        core == 0,
        jnp.concatenate([mine, received], axis=join_axis),
        jnp.concatenate([received, mine], axis=join_axis),
    )


def on_device(
    queries, keys_in, values_in, head_gain, master_weight, gradient, first_moment, second_moment
):
    moment_one = beta_one * first_moment + (1.0 - beta_one) * gradient
    moment_two = beta_two * second_moment + (1.0 - beta_two) * gradient * gradient
    corrected = (
        moment_one
        / (1.0 - beta_one**step_count)
        / (jnp.sqrt(moment_two / (1.0 - beta_two**step_count)) + adam_eps)
    )
    updated = master_weight - learn_rate * (corrected + decay_rate * master_weight)
    weights = updated.astype(jnp.bfloat16)
    tokens_here = queries.shape[1]
    seq_length = tokens_here * lax.axis_size(SEQ)
    half = lax.axis_index("xh")
    core = lax.axis_index("c")
    heads_here = H // 2
    halves = gather_first(weights)
    halves, query_heads = lax.optimization_barrier(
        (halves, queries[0].reshape(tokens_here, H, HEAD))
    )
    parts = gather_start(halves)
    query_group = pair_exchange(query_heads, core, 1, 0)
    sent = [ring_send(part, second, 4) for part, (_, second) in zip(parts, STAGES)]
    key_group = pair_exchange(keys_in[0].reshape(tokens_here, H, HEAD), core, 1, 0)
    value_group = pair_exchange(values_in[0].reshape(tokens_here, H, HEAD), core, 1, 0)
    span = query_group.shape[0]
    offset = half * span
    query_blocks = to_blocks(featurize(query_group, offset, seq_length))
    key_blocks = to_blocks(featurize(key_group, offset, seq_length))
    value_blocks = to_blocks(value_group)
    states = jnp.einsum(
        "cjhf,cjhe->chfe", key_blocks, value_blocks, preferred_element_type=jnp.float32
    )
    chip_total = jnp.sum(states, axis=0)
    sent, chip_total = lax.optimization_barrier((sent, chip_total))
    sent = [ring_far(received, second, 4) for received, (_, second) in zip(sent, STAGES)]
    earlier = lax.ppermute(chip_total, "xh", [(0, 1)])
    scores = jnp.einsum(
        "cihf,cjhf->chij", query_blocks, key_blocks, preferred_element_type=jnp.float32
    )
    causal_mask = jnp.arange(CH)[:, None] >= jnp.arange(CH)[None, :]
    scores = jnp.where(causal_mask[None, None], scores, 0.0).astype(jnp.bfloat16)
    inside_block = jnp.einsum(
        "chij,cjhe->cihe", scores, value_blocks, preferred_element_type=jnp.float32
    )
    running = jnp.cumsum(states, axis=0)
    local_before = jnp.concatenate([jnp.zeros_like(states[:1]), running[:-1]], axis=0)
    before = (earlier[None] + local_before).astype(jnp.bfloat16)
    from_before = jnp.einsum(
        "cihf,chfe->cihe", query_blocks, before, preferred_element_type=jnp.float32
    )
    attended = (inside_block + from_before).reshape(span, heads_here, HEAD)
    gain_rows = lax.dynamic_slice_in_dim(head_gain, core * heads_here, heads_here, 0)
    normed_group = normalize(attended, gain_rows)
    normed_own = pair_exchange(normed_group, core, 0, 1)
    normed_own = normed_own.reshape(tokens_here, H * HEAD)
    tokens = jnp.concatenate([normed_own, swap(normed_own, "c")], axis=0)
    sent, tokens = lax.optimization_barrier((sent, tokens))
    by_block = tokens.reshape(tokens.shape[0], 32, -1)
    wide = []
    for rows, source in gather_finish(parts, sent):
        features = jnp.take(by_block, source, axis=1).reshape(tokens.shape)
        wide.append(
            jnp.dot(features, rows, preferred_element_type=jnp.float32).astype(jnp.bfloat16)
        )
    own = [piece[:tokens_here] for piece in wide]
    returned = [swap(piece[tokens_here:], "c") for piece in wide]
    candidates = own + returned

    def place(chip, side):
        order = []
        for block in range(4):
            from_partner = (block % 2 - side) % 2
            order.append(2 * from_partner + (block // 2 - chip) % 2)
        return lambda *pieces: jnp.concatenate([pieces[i] for i in order], axis=1)

    branches = [place(chip, side) for chip in (0, 1) for side in (0, 1)]
    projected = lax.switch(half * 2 + core, branches, *candidates)
    layer_out = projected[None]
    return (layer_out, updated, moment_one, moment_two)


def solution(mesh):
    fine = Mesh(mesh.devices.reshape(4, 2, 4, 2, 2), DP + SEQ)
    data = P(DP, SEQ, None)
    blocks = P(DP, SEQ)
    in_specs = (data, data, data, P(), blocks, blocks, blocks, blocks)
    out_specs = (data, blocks, blocks, blocks)
    return jax.shard_map(
        on_device, mesh=fine, in_specs=in_specs, out_specs=out_specs, check_vma=False
    )
```

```python
import math

import jax
import jax.numpy as jnp
from jax import lax
from jax.sharding import Mesh, PartitionSpec as P

HEAD = 128
DP = ("z", "xl", "y")
SEQ = ("xh", "c")
H = 20
CH = 128


beta_one = 0.9
beta_two = 0.95
learn_rate = 0.0003
decay_rate = 0.1
adam_eps = 1e-08
step_count = 100
norm_eps = 1e-06


def ring_send(halves, axis, size):
    forward = [(k, (k + 1) % size) for k in range(size)]
    backward = [(k, (k - 1) % size) for k in range(size)]
    return tuple(lax.ppermute(half, axis, perm) for perm in (forward, backward) for half in halves)


def ring_far(received, axis, size):
    forward = [(k, (k + 1) % size) for k in range(size)]
    backward = [(k, (k - 1) % size) for k in range(size)]
    left_a, left_b, right_a, right_b = received
    far_a = lax.ppermute(left_a, axis, forward)
    far_b = lax.ppermute(right_b, axis, backward)
    return (left_a, left_b, far_a, far_b, right_a, right_b)


def ring_finish(halves, received):
    pieces = jnp.stack(tuple(halves) + tuple(received))
    return pieces.reshape((4, pieces.shape[1] * 2) + pieces.shape[2:])


STAGES = (("y", "z"), ("z", "y"))


def ring_direct(x, axis, size):
    shifted = [
        lax.ppermute(x, axis, [(k, (k + shift) % size) for k in range(size)])
        for shift in (1, 2, 3)
    ]
    return (jnp.stack([x, shifted[0]]), jnp.stack([shifted[1], shifted[2]]))


def gather_start(weights):
    near = swap(weights, "xl")
    peer = swap(weights, "xh")
    diagonal = lax.ppermute(weights, ("xl", "xh"), [(k, 3 - k) for k in range(4)])
    halves = (jnp.stack([weights, near]), jnp.stack([peer, diagonal]))
    return [ring_direct(part, first, 4) for part, (first, _) in zip(halves, STAGES)]


def gather_finish(parts, sent):
    z = lax.axis_index("z")
    xl = lax.axis_index("xl")
    y = lax.axis_index("y")
    stacked = jnp.arange(32)
    pieces = []
    for part, received, (first, _) in zip(parts, sent, STAGES):
        part = ring_finish(part, received)
        outer, inner, xl_rel = stacked // 8, (stacked // 2) % 4, stacked % 2
        z_rel, y_rel = (outer, inner) if first == "y" else (inner, outer)
        source = ((z - z_rel) % 4) * 8 + ((xl - xl_rel) % 2) * 4 + (y - y_rel) % 4
        pieces.append((part.reshape(-1, part.shape[-1]), source))
    return pieces


def seq_shift(x, shift):
    return lax.ppermute(x, SEQ, [(k, (k + shift) % 4) for k in range(4)])

def featurize(block, offset, seq_length):
    positions = (offset + jnp.arange(block.shape[0], dtype=jnp.int32)).astype(jnp.float32)
    angles = positions * (math.pi / (2.0 * seq_length))
    rectified = jnp.maximum(block.astype(jnp.float32), 0.0)
    cosine = rectified * jnp.cos(angles)[:, None, None]
    sine = rectified * jnp.sin(angles)[:, None, None]
    return jnp.concatenate([cosine, sine], axis=2).astype(jnp.bfloat16)


def to_blocks(x):
    return x.reshape((x.shape[0] // CH, CH) + x.shape[1:])


def normalize(attended, gain_rows):
    mean_square = jnp.mean(attended * attended, axis=2, keepdims=True)
    return (attended * lax.rsqrt(mean_square + norm_eps) * gain_rows[None]).astype(jnp.bfloat16)


def swap(x, axis):
    return lax.ppermute(x, axis, [(0, 1), (1, 0)])


def pair_exchange(x, core, keep_axis, join_axis):
    size = x.shape[keep_axis] // 2
    mine = lax.dynamic_slice_in_dim(x, core * size, size, keep_axis)
    theirs = lax.dynamic_slice_in_dim(x, (1 - core) * size, size, keep_axis)
    received = swap(theirs, "c")
    return jnp.where(
        core == 0,
        jnp.concatenate([mine, received], axis=join_axis),
        jnp.concatenate([received, mine], axis=join_axis),
    )


def on_device(
    queries, keys_in, values_in, head_gain, master_weight, gradient, first_moment, second_moment
):
    moment_one = beta_one * first_moment + (1.0 - beta_one) * gradient
    moment_two = beta_two * second_moment + (1.0 - beta_two) * gradient * gradient
    corrected = (
        moment_one
        / (1.0 - beta_one**step_count)
        / (jnp.sqrt(moment_two / (1.0 - beta_two**step_count)) + adam_eps)
    )
    updated = master_weight - learn_rate * (corrected + decay_rate * master_weight)
    weights = updated.astype(jnp.bfloat16)
    tokens_here = queries.shape[1]
    seq_length = tokens_here * lax.axis_size(SEQ)
    half = lax.axis_index("xh")
    core = lax.axis_index("c")
    heads_here = H // 2
    parts = gather_start(weights)
    parts, query_heads = lax.optimization_barrier(
        (parts, queries[0].reshape(tokens_here, H, HEAD))
    )
    query_group = pair_exchange(query_heads, core, 1, 0)
    sent = [ring_send(part, second, 4) for part, (_, second) in zip(parts, STAGES)]
    key_group = pair_exchange(keys_in[0].reshape(tokens_here, H, HEAD), core, 1, 0)
    value_group = pair_exchange(values_in[0].reshape(tokens_here, H, HEAD), core, 1, 0)
    span = query_group.shape[0]
    offset = half * span
    query_blocks = to_blocks(featurize(query_group, offset, seq_length))
    key_blocks = to_blocks(featurize(key_group, offset, seq_length))
    value_blocks = to_blocks(value_group)
    states = jnp.einsum(
        "cjhf,cjhe->chfe", key_blocks, value_blocks, preferred_element_type=jnp.float32
    )
    chip_total = jnp.sum(states, axis=0)
    sent, chip_total = lax.optimization_barrier((sent, chip_total))
    sent = [ring_far(received, second, 4) for received, (_, second) in zip(sent, STAGES)]
    earlier = lax.ppermute(chip_total, "xh", [(0, 1)])
    scores = jnp.einsum(
        "cihf,cjhf->chij", query_blocks, key_blocks, preferred_element_type=jnp.float32
    )
    causal_mask = jnp.arange(CH)[:, None] >= jnp.arange(CH)[None, :]
    scores = jnp.where(causal_mask[None, None], scores, 0.0).astype(jnp.bfloat16)
    inside_block = jnp.einsum(
        "chij,cjhe->cihe", scores, value_blocks, preferred_element_type=jnp.float32
    )
    running = jnp.cumsum(states, axis=0)
    local_before = jnp.concatenate([jnp.zeros_like(states[:1]), running[:-1]], axis=0)
    before = (earlier[None] + local_before).astype(jnp.bfloat16)
    from_before = jnp.einsum(
        "cihf,chfe->cihe", query_blocks, before, preferred_element_type=jnp.float32
    )
    attended = (inside_block + from_before).reshape(span, heads_here, HEAD)
    sent, attended = lax.optimization_barrier((sent, attended))
    gain_rows = lax.dynamic_slice_in_dim(head_gain, core * heads_here, heads_here, 0)
    normed_group = normalize(attended, gain_rows)
    normed_own = pair_exchange(normed_group, core, 0, 1)
    normed_own = normed_own.reshape(tokens_here, H * HEAD)
    tokens = jnp.concatenate([normed_own, swap(normed_own, "c")], axis=0)
    by_block = tokens.reshape(tokens.shape[0], 32, -1)
    wide = []
    for rows, source in gather_finish(parts, sent):
        features = jnp.take(by_block, source, axis=1).reshape(tokens.shape)
        wide.append(
            jnp.dot(features, rows, preferred_element_type=jnp.float32).astype(jnp.bfloat16)
        )
    own = [piece[:tokens_here] for piece in wide]
    returned = [swap(piece[tokens_here:], "c") for piece in wide]
    candidates = own + returned

    def place(chip, side):
        order = []
        for block in range(4):
            from_partner = (block % 2 - side) % 2
            order.append(2 * from_partner + (block // 2 - chip) % 2)
        return lambda *pieces: jnp.concatenate([pieces[i] for i in order], axis=1)

    branches = [place(chip, side) for chip in (0, 1) for side in (0, 1)]
    projected = lax.switch(half * 2 + core, branches, *candidates)
    layer_out = projected[None]
    return (layer_out, updated, moment_one, moment_two)


def solution(mesh):
    fine = Mesh(mesh.devices.reshape(4, 2, 4, 2, 2), DP + SEQ)
    data = P(DP, SEQ, None)
    blocks = P(DP, SEQ)
    in_specs = (data, data, data, P(), blocks, blocks, blocks, blocks)
    out_specs = (data, blocks, blocks, blocks)
    return jax.shard_map(
        on_device, mesh=fine, in_specs=in_specs, out_specs=out_specs, check_vma=False
    )
```

```python
import math

import jax
import jax.numpy as jnp
from jax import lax
from jax.sharding import Mesh, PartitionSpec as P

HEAD = 128
DP = ("z", "xl", "y")
SEQ = ("xh", "c")
H = 20
CH = 128


beta_one = 0.9
beta_two = 0.95
learn_rate = 0.0003
decay_rate = 0.1
adam_eps = 1e-08
step_count = 100
norm_eps = 1e-06


def ring_send(x, axis, size):
    if size == 2:
        return (lax.ppermute(x, axis, [(0, 1), (1, 0)]),)
    forward = [(k, (k + 1) % size) for k in range(size)]
    backward = [(k, (k - 1) % size) for k in range(size)]
    return (lax.ppermute(x, axis, forward), lax.ppermute(x, axis, backward))


def ring_far(received, axis, size):
    if size == 2:
        return received
    forward = [(k, (k + 1) % size) for k in range(size)]
    backward = [(k, (k - 1) % size) for k in range(size)]
    from_left, from_right = received
    half = from_left.shape[0] // 2
    far = jnp.concatenate(
        [
            lax.ppermute(from_left[:half], axis, forward),
            lax.ppermute(from_right[half:], axis, backward),
        ],
        axis=0,
    )
    return (from_left, far, from_right)


def ring_finish(x, received):
    return jnp.stack((x,) + tuple(received))


def ring_gather(x, axis, size):
    return ring_finish(x, ring_far(ring_send(x, axis, size), axis, size))


STAGES = (("y", "z"), ("z", "y"))


def ring_direct(x, axis, size):
    shifted = [
        lax.ppermute(x, axis, [(k, (k + shift) % size) for k in range(size)])
        for shift in (1, 2, 3)
    ]
    return jnp.stack([x] + shifted)


def gather_start(weights):
    near = swap(weights, "xl")
    peer = swap(weights, "xh")
    diagonal = lax.ppermute(weights, ("xl", "xh"), [(k, 3 - k) for k in range(4)])
    halves = (jnp.stack([weights, near]), jnp.stack([peer, diagonal]))
    return [ring_direct(part, first, 4) for part, (first, _) in zip(halves, STAGES)]


def gather_finish(parts, sent):
    z = lax.axis_index("z")
    xl = lax.axis_index("xl")
    y = lax.axis_index("y")
    stacked = jnp.arange(32)
    pieces = []
    for part, received, (first, _) in zip(parts, sent, STAGES):
        part = ring_finish(part, received)
        outer, inner, xl_rel = stacked // 8, (stacked // 2) % 4, stacked % 2
        z_rel, y_rel = (outer, inner) if first == "y" else (inner, outer)
        source = ((z - z_rel) % 4) * 8 + ((xl - xl_rel) % 2) * 4 + (y - y_rel) % 4
        pieces.append((part.reshape(-1, part.shape[-1]), source))
    return pieces


def seq_shift(x, shift):
    return lax.ppermute(x, SEQ, [(k, (k + shift) % 4) for k in range(4)])

def featurize(block, offset, seq_length):
    positions = (offset + jnp.arange(block.shape[0], dtype=jnp.int32)).astype(jnp.float32)
    angles = positions * (math.pi / (2.0 * seq_length))
    rectified = jnp.maximum(block.astype(jnp.float32), 0.0)
    cosine = rectified * jnp.cos(angles)[:, None, None]
    sine = rectified * jnp.sin(angles)[:, None, None]
    return jnp.concatenate([cosine, sine], axis=2).astype(jnp.bfloat16)


def to_blocks(x):
    return x.reshape((x.shape[0] // CH, CH) + x.shape[1:])


def normalize(attended, gain_rows):
    mean_square = jnp.mean(attended * attended, axis=2, keepdims=True)
    return (attended * lax.rsqrt(mean_square + norm_eps) * gain_rows[None]).astype(jnp.bfloat16)


def swap(x, axis):
    return lax.ppermute(x, axis, [(0, 1), (1, 0)])


def pair_exchange(x, core, keep_axis, join_axis):
    size = x.shape[keep_axis] // 2
    mine = lax.dynamic_slice_in_dim(x, core * size, size, keep_axis)
    theirs = lax.dynamic_slice_in_dim(x, (1 - core) * size, size, keep_axis)
    received = swap(theirs, "c")
    length = mine.shape[join_axis]
    shape = list(mine.shape)
    shape[join_axis] = 2 * length
    joined = jnp.zeros(shape, mine.dtype)
    joined = lax.dynamic_update_slice_in_dim(joined, mine, core * length, join_axis)
    return lax.dynamic_update_slice_in_dim(joined, received, (1 - core) * length, join_axis)


def on_device(
    queries, keys_in, values_in, head_gain, master_weight, gradient, first_moment, second_moment
):
    moment_one = beta_one * first_moment + (1.0 - beta_one) * gradient
    moment_two = beta_two * second_moment + (1.0 - beta_two) * gradient * gradient
    corrected = (
        moment_one
        / (1.0 - beta_one**step_count)
        / (jnp.sqrt(moment_two / (1.0 - beta_two**step_count)) + adam_eps)
    )
    updated = master_weight - learn_rate * (corrected + decay_rate * master_weight)
    weights = updated.astype(jnp.bfloat16)
    tokens_here = queries.shape[1]
    seq_length = tokens_here * lax.axis_size(SEQ)
    half = lax.axis_index("xh")
    core = lax.axis_index("c")
    heads_here = H // 2
    parts = gather_start(weights)
    parts, query_heads = lax.optimization_barrier(
        (parts, queries[0].reshape(tokens_here, H, HEAD))
    )
    query_group = pair_exchange(query_heads, core, 1, 0)
    sent = [ring_send(part, second, 4) for part, (_, second) in zip(parts, STAGES)]
    key_group = pair_exchange(keys_in[0].reshape(tokens_here, H, HEAD), core, 1, 0)
    value_group = pair_exchange(values_in[0].reshape(tokens_here, H, HEAD), core, 1, 0)
    span = query_group.shape[0]
    offset = half * span
    query_blocks = to_blocks(featurize(query_group, offset, seq_length))
    key_blocks = to_blocks(featurize(key_group, offset, seq_length))
    value_blocks = to_blocks(value_group)
    states = jnp.einsum(
        "cjhf,cjhe->chfe", key_blocks, value_blocks, preferred_element_type=jnp.float32
    )
    chip_total = jnp.sum(states, axis=0)
    sent, chip_total = lax.optimization_barrier((sent, chip_total))
    sent = [ring_far(received, second, 4) for received, (_, second) in zip(sent, STAGES)]
    earlier = lax.ppermute(chip_total, "xh", [(0, 1)])
    scores = jnp.einsum(
        "cihf,cjhf->chij", query_blocks, key_blocks, preferred_element_type=jnp.float32
    )
    causal_mask = jnp.arange(CH)[:, None] >= jnp.arange(CH)[None, :]
    scores = jnp.where(causal_mask[None, None], scores, 0.0).astype(jnp.bfloat16)
    inside_block = jnp.einsum(
        "chij,cjhe->cihe", scores, value_blocks, preferred_element_type=jnp.float32
    )
    running = jnp.cumsum(states, axis=0)
    local_before = jnp.concatenate([jnp.zeros_like(states[:1]), running[:-1]], axis=0)
    before = (earlier[None] + local_before).astype(jnp.bfloat16)
    from_before = jnp.einsum(
        "cihf,chfe->cihe", query_blocks, before, preferred_element_type=jnp.float32
    )
    attended = (inside_block + from_before).reshape(span, heads_here, HEAD)
    sent, attended = lax.optimization_barrier((sent, attended))
    gain_rows = lax.dynamic_slice_in_dim(head_gain, core * heads_here, heads_here, 0)
    normed_group = normalize(attended, gain_rows)
    normed_own = pair_exchange(normed_group, core, 0, 1)
    normed_own = normed_own.reshape(tokens_here, H * HEAD)
    tokens = jnp.concatenate([normed_own, swap(normed_own, "c")], axis=0)
    by_block = tokens.reshape(tokens.shape[0], 32, -1)
    wide = []
    for rows, source in gather_finish(parts, sent):
        features = jnp.take(by_block, source, axis=1).reshape(tokens.shape)
        wide.append(
            jnp.dot(features, rows, preferred_element_type=jnp.float32).astype(jnp.bfloat16)
        )
    own = [piece[:tokens_here] for piece in wide]
    returned = [swap(piece[tokens_here:], "c") for piece in wide]
    candidates = own + returned

    def place(chip, side):
        order = []
        for block in range(4):
            from_partner = (block % 2 - side) % 2
            order.append(2 * from_partner + (block // 2 - chip) % 2)
        return lambda *pieces: jnp.concatenate([pieces[i] for i in order], axis=1)

    branches = [place(chip, side) for chip in (0, 1) for side in (0, 1)]
    projected = lax.switch(half * 2 + core, branches, *candidates)
    layer_out = projected[None]
    return (layer_out, updated, moment_one, moment_two)


def solution(mesh):
    fine = Mesh(mesh.devices.reshape(4, 2, 4, 2, 2), DP + SEQ)
    data = P(DP, SEQ, None)
    blocks = P(DP, SEQ)
    in_specs = (data, data, data, P(), blocks, blocks, blocks, blocks)
    out_specs = (data, blocks, blocks, blocks)
    return jax.shard_map(
        on_device, mesh=fine, in_specs=in_specs, out_specs=out_specs, check_vma=False
    )
```

```python
import math

import jax
import jax.numpy as jnp
from jax import lax
from jax.sharding import Mesh, PartitionSpec as P

HEAD = 128
DP = ("z", "xl", "y")
SEQ = ("xh", "c")
H = 20
CH = 128


beta_one = 0.9
beta_two = 0.95
learn_rate = 0.0003
decay_rate = 0.1
adam_eps = 1e-08
step_count = 100
norm_eps = 1e-06


def ring_send(x, axis, size):
    if size == 2:
        return (lax.ppermute(x, axis, [(0, 1), (1, 0)]),)
    forward = [(k, (k + 1) % size) for k in range(size)]
    backward = [(k, (k - 1) % size) for k in range(size)]
    return (lax.ppermute(x, axis, forward), lax.ppermute(x, axis, backward))


def ring_far(received, axis, size):
    if size == 2:
        return received
    forward = [(k, (k + 1) % size) for k in range(size)]
    backward = [(k, (k - 1) % size) for k in range(size)]
    from_left, from_right = received
    half = from_left.shape[0] // 2
    far = jnp.concatenate(
        [
            lax.ppermute(from_left[:half], axis, forward),
            lax.ppermute(from_right[half:], axis, backward),
        ],
        axis=0,
    )
    return (from_left, far, from_right)


def ring_finish(x, received):
    return jnp.stack((x,) + tuple(received))


def ring_gather(x, axis, size):
    return ring_finish(x, ring_far(ring_send(x, axis, size), axis, size))


STAGES = (("y", "z"), ("z", "y"))


def ring_direct(x, axis, size):
    shifted = [
        lax.ppermute(x, axis, [(k, (k + shift) % size) for k in range(size)])
        for shift in (1, 2, 3)
    ]
    return jnp.stack([x] + shifted)


def gather_first(weights):
    near = swap(weights, "xl")
    peer = swap(weights, "xh")
    diagonal = lax.ppermute(weights, ("xl", "xh"), [(k, 3 - k) for k in range(4)])
    return (jnp.stack([weights, near]), jnp.stack([peer, diagonal]))


def gather_start(halves):
    return [ring_direct(part, first, 4) for part, (first, _) in zip(halves, STAGES)]


def gather_finish(parts, sent):
    z = lax.axis_index("z")
    xl = lax.axis_index("xl")
    y = lax.axis_index("y")
    stacked = jnp.arange(32)
    pieces = []
    for part, received, (first, _) in zip(parts, sent, STAGES):
        part = ring_finish(part, received)
        outer, inner, xl_rel = stacked // 8, (stacked // 2) % 4, stacked % 2
        z_rel, y_rel = (outer, inner) if first == "y" else (inner, outer)
        source = ((z - z_rel) % 4) * 8 + ((xl - xl_rel) % 2) * 4 + (y - y_rel) % 4
        pieces.append((part.reshape(-1, part.shape[-1]), source))
    return pieces


def seq_shift(x, shift):
    return lax.ppermute(x, SEQ, [(k, (k + shift) % 4) for k in range(4)])

def featurize(block, offset, seq_length):
    positions = (offset + jnp.arange(block.shape[0], dtype=jnp.int32)).astype(jnp.float32)
    angles = positions * (math.pi / (2.0 * seq_length))
    rectified = jnp.maximum(block.astype(jnp.float32), 0.0)
    cosine = rectified * jnp.cos(angles)[:, None, None]
    sine = rectified * jnp.sin(angles)[:, None, None]
    return jnp.concatenate([cosine, sine], axis=2).astype(jnp.bfloat16)


def to_blocks(x):
    return x.reshape((x.shape[0] // CH, CH) + x.shape[1:])


def normalize(attended, gain_rows):
    mean_square = jnp.mean(attended * attended, axis=2, keepdims=True)
    return (attended * lax.rsqrt(mean_square + norm_eps) * gain_rows[None]).astype(jnp.bfloat16)


def swap(x, axis):
    return lax.ppermute(x, axis, [(0, 1), (1, 0)])


def pair_exchange(x, core, keep_axis, join_axis):
    size = x.shape[keep_axis] // 2
    mine = lax.dynamic_slice_in_dim(x, core * size, size, keep_axis)
    theirs = lax.dynamic_slice_in_dim(x, (1 - core) * size, size, keep_axis)
    received = swap(theirs, "c")
    return jnp.where(
        core == 0,
        jnp.concatenate([mine, received], axis=join_axis),
        jnp.concatenate([received, mine], axis=join_axis),
    )


def on_device(
    queries, keys_in, values_in, head_gain, master_weight, gradient, first_moment, second_moment
):
    moment_one = beta_one * first_moment + (1.0 - beta_one) * gradient
    moment_two = beta_two * second_moment + (1.0 - beta_two) * gradient * gradient
    corrected = (
        moment_one
        / (1.0 - beta_one**step_count)
        / (jnp.sqrt(moment_two / (1.0 - beta_two**step_count)) + adam_eps)
    )
    updated = master_weight - learn_rate * (corrected + decay_rate * master_weight)
    weights = updated.astype(jnp.bfloat16)
    tokens_here = queries.shape[1]
    seq_length = tokens_here * lax.axis_size(SEQ)
    half = lax.axis_index("xh")
    core = lax.axis_index("c")
    heads_here = H // 2
    halves = gather_first(weights)
    halves, query_heads = lax.optimization_barrier(
        (halves, queries[0].reshape(tokens_here, H, HEAD))
    )
    parts = gather_start(halves)
    query_group = pair_exchange(query_heads, core, 1, 0)
    sent = [ring_send(part, second, 4) for part, (_, second) in zip(parts, STAGES)]
    key_group = pair_exchange(keys_in[0].reshape(tokens_here, H, HEAD), core, 1, 0)
    value_group = pair_exchange(values_in[0].reshape(tokens_here, H, HEAD), core, 1, 0)
    span = query_group.shape[0]
    offset = half * span
    query_blocks = to_blocks(featurize(query_group, offset, seq_length))
    key_blocks = to_blocks(featurize(key_group, offset, seq_length))
    value_blocks = to_blocks(value_group)
    states = jnp.einsum(
        "cjhf,cjhe->chfe", key_blocks, value_blocks, preferred_element_type=jnp.float32
    )
    chip_total = jnp.sum(states, axis=0)
    sent, chip_total = lax.optimization_barrier((sent, chip_total))
    sent = [ring_far(received, second, 4) for received, (_, second) in zip(sent, STAGES)]
    earlier = lax.ppermute(chip_total, "xh", [(0, 1)])
    scores = jnp.einsum(
        "cihf,cjhf->chij", query_blocks, key_blocks, preferred_element_type=jnp.float32
    )
    causal_mask = jnp.arange(CH)[:, None] >= jnp.arange(CH)[None, :]
    scores = jnp.where(causal_mask[None, None], scores, 0.0).astype(jnp.bfloat16)
    inside_block = jnp.einsum(
        "chij,cjhe->cihe", scores, value_blocks, preferred_element_type=jnp.float32
    )
    running = jnp.cumsum(states, axis=0)
    local_before = jnp.concatenate([jnp.zeros_like(states[:1]), running[:-1]], axis=0)
    before = (earlier[None] + local_before).astype(jnp.bfloat16)
    from_before = jnp.einsum(
        "cihf,chfe->cihe", query_blocks, before, preferred_element_type=jnp.float32
    )
    attended = (inside_block + from_before).reshape(span, heads_here, HEAD)
    sent, attended = lax.optimization_barrier((sent, attended))
    gain_rows = lax.dynamic_slice_in_dim(head_gain, core * heads_here, heads_here, 0)
    normed_group = normalize(attended, gain_rows)
    normed_own = pair_exchange(normed_group, core, 0, 1)
    normed_own = normed_own.reshape(tokens_here, H * HEAD)
    tokens = jnp.concatenate([normed_own, swap(normed_own, "c")], axis=0)
    by_block = tokens.reshape(tokens.shape[0], 32, -1)
    wide = []
    for rows, source in gather_finish(parts, sent):
        features = jnp.take(by_block, source, axis=1).reshape(tokens.shape)
        wide.append(
            jnp.dot(features, rows, preferred_element_type=jnp.float32).astype(jnp.bfloat16)
        )
    own = [piece[:tokens_here] for piece in wide]
    returned = [swap(piece[tokens_here:], "c") for piece in wide]
    candidates = own + returned

    def place(chip, side):
        order = []
        for block in range(4):
            from_partner = (block % 2 - side) % 2
            order.append(2 * from_partner + (block // 2 - chip) % 2)
        return lambda *pieces: jnp.concatenate([pieces[i] for i in order], axis=1)

    branches = [place(chip, side) for chip in (0, 1) for side in (0, 1)]
    projected = lax.switch(half * 2 + core, branches, *candidates)
    layer_out = projected[None]
    return (layer_out, updated, moment_one, moment_two)


def solution(mesh):
    fine = Mesh(mesh.devices.reshape(4, 2, 4, 2, 2), DP + SEQ)
    data = P(DP, SEQ, None)
    blocks = P(DP, SEQ)
    in_specs = (data, data, data, P(), blocks, blocks, blocks, blocks)
    out_specs = (data, blocks, blocks, blocks)
    return jax.shard_map(
        on_device, mesh=fine, in_specs=in_specs, out_specs=out_specs, check_vma=False
    )
```

```python
import math

import jax
import jax.numpy as jnp
from jax import lax
from jax.sharding import Mesh, PartitionSpec as P

HEAD = 128
DP = ("z", "xl", "y")
SEQ = ("xh", "c")
H = 20
CH = 128


beta_one = 0.9
beta_two = 0.95
learn_rate = 0.0003
decay_rate = 0.1
adam_eps = 1e-08
step_count = 100
norm_eps = 1e-06


def ring_send(x, axis, size):
    if size == 2:
        return (lax.ppermute(x, axis, [(0, 1), (1, 0)]),)
    forward = [(k, (k + 1) % size) for k in range(size)]
    backward = [(k, (k - 1) % size) for k in range(size)]
    return (lax.ppermute(x, axis, forward), lax.ppermute(x, axis, backward))


def ring_far(received, axis, size):
    if size == 2:
        return received
    forward = [(k, (k + 1) % size) for k in range(size)]
    backward = [(k, (k - 1) % size) for k in range(size)]
    from_left, from_right = received
    half = from_left.shape[0] // 2
    far = jnp.concatenate(
        [
            lax.ppermute(from_left[:half], axis, forward),
            lax.ppermute(from_right[half:], axis, backward),
        ],
        axis=0,
    )
    return (from_left, far, from_right)


def ring_finish(x, received):
    return jnp.stack((x,) + tuple(received))


def ring_gather(x, axis, size):
    return ring_finish(x, ring_far(ring_send(x, axis, size), axis, size))


STAGES = (("y", "z"), ("z", "y"))


def ring_direct(x, axis, size):
    shifted = [
        lax.ppermute(x, axis, [(k, (k + shift) % size) for k in range(size)])
        for shift in (1, 2, 3)
    ]
    return jnp.stack([x] + shifted)


def gather_start(weights):
    near = swap(weights, "xl")
    peer = swap(weights, "xh")
    diagonal = lax.ppermute(weights, ("xl", "xh"), [(k, 3 - k) for k in range(4)])
    halves = (jnp.stack([weights, near]), jnp.stack([peer, diagonal]))
    return [ring_direct(part, first, 4) for part, (first, _) in zip(halves, STAGES)]


def gather_finish(parts, sent):
    z = lax.axis_index("z")
    xl = lax.axis_index("xl")
    y = lax.axis_index("y")
    stacked = jnp.arange(32)
    pieces = []
    for part, received, (first, _) in zip(parts, sent, STAGES):
        part = ring_finish(part, received)
        outer, inner, xl_rel = stacked // 8, (stacked // 2) % 4, stacked % 2
        z_rel, y_rel = (outer, inner) if first == "y" else (inner, outer)
        source = ((z - z_rel) % 4) * 8 + ((xl - xl_rel) % 2) * 4 + (y - y_rel) % 4
        pieces.append((part.reshape(-1, part.shape[-1]), source))
    return pieces


def seq_shift(x, shift):
    return lax.ppermute(x, SEQ, [(k, (k + shift) % 4) for k in range(4)])

def featurize(block, offset, seq_length):
    positions = (offset + jnp.arange(block.shape[0], dtype=jnp.int32)).astype(jnp.float32)
    angles = positions * (math.pi / (2.0 * seq_length))
    rectified = jnp.maximum(block.astype(jnp.float32), 0.0)
    cosine = rectified * jnp.cos(angles)[:, None, None]
    sine = rectified * jnp.sin(angles)[:, None, None]
    return jnp.concatenate([cosine, sine], axis=2).astype(jnp.bfloat16)


def to_blocks(x):
    return x.reshape((x.shape[0] // CH, CH) + x.shape[1:])


def normalize(attended, gain_rows):
    mean_square = jnp.mean(attended * attended, axis=2, keepdims=True)
    return (attended * lax.rsqrt(mean_square + norm_eps) * gain_rows[None]).astype(jnp.bfloat16)


def swap(x, axis):
    return lax.ppermute(x, axis, [(0, 1), (1, 0)])


def pair_exchange(x, core, keep_axis, join_axis):
    size = x.shape[keep_axis] // 2
    mine = lax.dynamic_slice_in_dim(x, core * size, size, keep_axis)
    theirs = lax.dynamic_slice_in_dim(x, (1 - core) * size, size, keep_axis)
    received = swap(theirs, "c")
    return jnp.where(
        core == 0,
        jnp.concatenate([mine, received], axis=join_axis),
        jnp.concatenate([received, mine], axis=join_axis),
    )


def on_device(
    queries, keys_in, values_in, head_gain, master_weight, gradient, first_moment, second_moment
):
    moment_one = beta_one * first_moment + (1.0 - beta_one) * gradient
    moment_two = beta_two * second_moment + (1.0 - beta_two) * gradient * gradient
    corrected = (
        moment_one
        / (1.0 - beta_one**step_count)
        / (jnp.sqrt(moment_two / (1.0 - beta_two**step_count)) + adam_eps)
    )
    updated = master_weight - learn_rate * (corrected + decay_rate * master_weight)
    weights = updated.astype(jnp.bfloat16)
    tokens_here = queries.shape[1]
    seq_length = tokens_here * lax.axis_size(SEQ)
    half = lax.axis_index("xh")
    core = lax.axis_index("c")
    heads_here = H // 2
    parts = gather_start(weights)
    parts, query_heads = lax.optimization_barrier(
        (parts, queries[0].reshape(tokens_here, H, HEAD))
    )
    query_group = pair_exchange(query_heads, core, 1, 0)
    sent = [ring_send(part, second, 4) for part, (_, second) in zip(parts, STAGES)]
    key_group = pair_exchange(keys_in[0].reshape(tokens_here, H, HEAD), core, 1, 0)
    value_group = pair_exchange(values_in[0].reshape(tokens_here, H, HEAD), core, 1, 0)
    span = query_group.shape[0]
    offset = half * span
    query_blocks = to_blocks(featurize(query_group, offset, seq_length))
    key_blocks = to_blocks(featurize(key_group, offset, seq_length))
    value_blocks = to_blocks(value_group)
    states = jnp.einsum(
        "cjhf,cjhe->chfe", key_blocks, value_blocks, preferred_element_type=jnp.float32
    )
    chip_total = jnp.sum(states, axis=0)
    sent, chip_total = lax.optimization_barrier((sent, chip_total))
    sent = [ring_far(received, second, 4) for received, (_, second) in zip(sent, STAGES)]
    earlier = lax.ppermute(chip_total, "xh", [(0, 1)])
    scores = jnp.einsum(
        "cihf,cjhf->chij", query_blocks, key_blocks, preferred_element_type=jnp.float32
    )
    causal_mask = jnp.arange(CH)[:, None] >= jnp.arange(CH)[None, :]
    scores = jnp.where(causal_mask[None, None], scores, 0.0).astype(jnp.bfloat16)
    inside_block = jnp.einsum(
        "chij,cjhe->cihe", scores, value_blocks, preferred_element_type=jnp.float32
    )
    running = jnp.cumsum(states, axis=0)
    local_before = jnp.concatenate([jnp.zeros_like(states[:1]), running[:-1]], axis=0)
    before = (earlier[None] + local_before).astype(jnp.bfloat16)
    from_before = jnp.einsum(
        "cihf,chfe->cihe", query_blocks, before, preferred_element_type=jnp.float32
    )
    attended = (inside_block + from_before).reshape(span, heads_here, HEAD)
    sent, attended = lax.optimization_barrier((sent, attended))
    gain_rows = lax.dynamic_slice_in_dim(head_gain, core * heads_here, heads_here, 0)
    normed_group = normalize(attended, gain_rows)
    normed_own = pair_exchange(normed_group, core, 0, 1)
    normed_own = normed_own.reshape(tokens_here, H * HEAD)
    tokens = jnp.concatenate([normed_own, swap(normed_own, "c")], axis=0)
    by_block = tokens.reshape(tokens.shape[0], 32, -1)
    wide = []
    for rows, source in gather_finish(parts, sent):
        features = jnp.take(by_block, source, axis=1, mode="clip").reshape(tokens.shape)
        wide.append(
            jnp.dot(features, rows, preferred_element_type=jnp.float32).astype(jnp.bfloat16)
        )
    own = [piece[:tokens_here] for piece in wide]
    returned = [swap(piece[tokens_here:], "c") for piece in wide]
    candidates = own + returned

    def place(chip, side):
        order = []
        for block in range(4):
            from_partner = (block % 2 - side) % 2
            order.append(2 * from_partner + (block // 2 - chip) % 2)
        return lambda *pieces: jnp.concatenate([pieces[i] for i in order], axis=1)

    branches = [place(chip, side) for chip in (0, 1) for side in (0, 1)]
    projected = lax.switch(half * 2 + core, branches, *candidates)
    layer_out = projected[None]
    return (layer_out, updated, moment_one, moment_two)


def solution(mesh):
    fine = Mesh(mesh.devices.reshape(4, 2, 4, 2, 2), DP + SEQ)
    data = P(DP, SEQ, None)
    blocks = P(DP, SEQ)
    in_specs = (data, data, data, P(), blocks, blocks, blocks, blocks)
    out_specs = (data, blocks, blocks, blocks)
    return jax.shard_map(
        on_device, mesh=fine, in_specs=in_specs, out_specs=out_specs, check_vma=False
    )
```

```python
import math

import jax
import jax.numpy as jnp
from jax import lax
from jax.sharding import Mesh, PartitionSpec as P

HEAD = 128
DP = ("z", "xl", "y")
SEQ = ("xh", "c")
H = 20
CH = 128


beta_one = 0.9
beta_two = 0.95
learn_rate = 0.0003
decay_rate = 0.1
adam_eps = 1e-08
step_count = 100
norm_eps = 1e-06


def ring_send(x, axis, size):
    if size == 2:
        return (lax.ppermute(x, axis, [(0, 1), (1, 0)]),)
    forward = [(k, (k + 1) % size) for k in range(size)]
    backward = [(k, (k - 1) % size) for k in range(size)]
    return (lax.ppermute(x, axis, forward), lax.ppermute(x, axis, backward))


def ring_far(received, axis, size):
    if size == 2:
        return received
    forward = [(k, (k + 1) % size) for k in range(size)]
    backward = [(k, (k - 1) % size) for k in range(size)]
    from_left, from_right = received
    half = from_left.shape[0] // 2
    far = jnp.concatenate(
        [
            lax.ppermute(from_left[:half], axis, forward),
            lax.ppermute(from_right[half:], axis, backward),
        ],
        axis=0,
    )
    return (from_left, far, from_right)


def ring_finish(x, received):
    return jnp.stack((x,) + tuple(received))


def ring_gather(x, axis, size):
    return ring_finish(x, ring_far(ring_send(x, axis, size), axis, size))


STAGES = (("y", "z"), ("z", "y"))


def ring_direct(x, axis, size):
    shifted = [
        lax.ppermute(x, axis, [(k, (k + shift) % size) for k in range(size)])
        for shift in (1, 2, 3)
    ]
    return jnp.stack([x] + shifted)


def gather_start(weights):
    near = swap(weights, "xl")
    peer = swap(weights, "xh")
    diagonal = lax.ppermute(weights, ("xl", "xh"), [(k, 3 - k) for k in range(4)])
    halves = (jnp.stack([weights, near]), jnp.stack([peer, diagonal]))
    return [ring_direct(part, first, 4) for part, (first, _) in zip(halves, STAGES)]


def gather_finish(parts, sent):
    z = lax.axis_index("z")
    xl = lax.axis_index("xl")
    y = lax.axis_index("y")
    stacked = jnp.arange(32)
    pieces = []
    for part, received, (first, _) in zip(parts, sent, STAGES):
        part = ring_finish(part, received)
        outer, inner, xl_rel = stacked // 8, (stacked // 2) % 4, stacked % 2
        z_rel, y_rel = (outer, inner) if first == "y" else (inner, outer)
        source = ((z - z_rel) % 4) * 8 + ((xl - xl_rel) % 2) * 4 + (y - y_rel) % 4
        pieces.append((part.reshape(-1, part.shape[-1]), source))
    return pieces


def seq_shift(x, shift):
    return lax.ppermute(x, SEQ, [(k, (k + shift) % 4) for k in range(4)])

def featurize(block, offset, seq_length):
    positions = (offset + jnp.arange(block.shape[0], dtype=jnp.int32)).astype(jnp.float32)
    angles = positions * (math.pi / (2.0 * seq_length))
    rectified = jnp.maximum(block.astype(jnp.float32), 0.0)
    cosine = rectified * jnp.cos(angles)[:, None, None]
    sine = rectified * jnp.sin(angles)[:, None, None]
    return jnp.concatenate([cosine, sine], axis=2).astype(jnp.bfloat16)


def to_blocks(x):
    return x.reshape((x.shape[0] // CH, CH) + x.shape[1:])


def normalize(attended, gain_rows):
    mean_square = jnp.mean(attended * attended, axis=2, keepdims=True)
    return (attended * lax.rsqrt(mean_square + norm_eps) * gain_rows[None]).astype(jnp.bfloat16)


def swap(x, axis):
    return lax.ppermute(x, axis, [(0, 1), (1, 0)])


def pair_exchange(x, core, keep_axis, join_axis):
    size = x.shape[keep_axis] // 2
    mine = lax.dynamic_slice_in_dim(x, core * size, size, keep_axis)
    theirs = lax.dynamic_slice_in_dim(x, (1 - core) * size, size, keep_axis)
    received = swap(theirs, "c")
    return jnp.where(
        core == 0,
        jnp.concatenate([mine, received], axis=join_axis),
        jnp.concatenate([received, mine], axis=join_axis),
    )


def on_device(
    queries, keys_in, values_in, head_gain, master_weight, gradient, first_moment, second_moment
):
    moment_one = beta_one * first_moment + (1.0 - beta_one) * gradient
    moment_two = beta_two * second_moment + (1.0 - beta_two) * gradient * gradient
    corrected = (
        moment_one
        / (1.0 - beta_one**step_count)
        / (jnp.sqrt(moment_two / (1.0 - beta_two**step_count)) + adam_eps)
    )
    updated = master_weight - learn_rate * (corrected + decay_rate * master_weight)
    weights = updated.astype(jnp.bfloat16)
    tokens_here = queries.shape[1]
    seq_length = tokens_here * lax.axis_size(SEQ)
    half = lax.axis_index("xh")
    core = lax.axis_index("c")
    heads_here = H // 2
    parts = gather_start(weights)
    parts, query_heads = lax.optimization_barrier(
        (parts, queries[0].reshape(tokens_here, H, HEAD))
    )
    query_group = pair_exchange(query_heads, core, 1, 0)
    sent = [ring_send(part, second, 4) for part, (_, second) in zip(parts, STAGES)]
    key_group = pair_exchange(keys_in[0].reshape(tokens_here, H, HEAD), core, 1, 0)
    value_group = pair_exchange(values_in[0].reshape(tokens_here, H, HEAD), core, 1, 0)
    span = query_group.shape[0]
    offset = half * span
    query_blocks = to_blocks(featurize(query_group, offset, seq_length))
    key_blocks = to_blocks(featurize(key_group, offset, seq_length))
    value_blocks = to_blocks(value_group)
    states = jnp.einsum(
        "cjhf,cjhe->chfe", key_blocks, value_blocks, preferred_element_type=jnp.float32
    )
    chip_total = jnp.sum(states, axis=0)
    sent, chip_total = lax.optimization_barrier((sent, chip_total))
    sent = [ring_far(received, second, 4) for received, (_, second) in zip(sent, STAGES)]
    earlier = lax.ppermute(chip_total, "xh", [(0, 1)])
    scores = jnp.einsum(
        "cihf,cjhf->chij", query_blocks, key_blocks, preferred_element_type=jnp.float32
    )
    causal_mask = jnp.arange(CH)[:, None] >= jnp.arange(CH)[None, :]
    scores = jnp.where(causal_mask[None, None], scores, 0.0).astype(jnp.bfloat16)
    inside_block = jnp.einsum(
        "chij,cjhe->cihe", scores, value_blocks, preferred_element_type=jnp.float32
    )
    running = jnp.cumsum(states, axis=0)
    local_before = jnp.concatenate([jnp.zeros_like(states[:1]), running[:-1]], axis=0)
    before = (earlier[None] + local_before).astype(jnp.bfloat16)
    from_before = jnp.einsum(
        "cihf,chfe->cihe", query_blocks, before, preferred_element_type=jnp.float32
    )
    attended = (inside_block + from_before).reshape(span, heads_here, HEAD)
    sent, attended = lax.optimization_barrier((sent, attended))
    gain_rows = lax.dynamic_slice_in_dim(head_gain, core * heads_here, heads_here, 0)
    normed_group = normalize(attended, gain_rows)
    normed_own = pair_exchange(normed_group, core, 0, 1)
    normed_own = normed_own.reshape(tokens_here, H * HEAD)
    tokens = jnp.concatenate([normed_own, swap(normed_own, "c")], axis=0)
    by_block = tokens.reshape(tokens.shape[0], 32, -1)
    wide = []
    for rows, source in gather_finish(parts, sent):
        features = jnp.take(by_block, source, axis=1, mode="clip").reshape(tokens.shape)
        wide.append(
            jnp.dot(features, rows, preferred_element_type=jnp.float32).astype(jnp.bfloat16)
        )
    own = [piece[:tokens_here] for piece in wide]
    returned = swap(jnp.stack([piece[tokens_here:] for piece in wide]), "c")
    returned = [returned[0], returned[1]]
    candidates = own + returned

    def place(chip, side):
        order = []
        for block in range(4):
            from_partner = (block % 2 - side) % 2
            order.append(2 * from_partner + (block // 2 - chip) % 2)
        return lambda *pieces: jnp.concatenate([pieces[i] for i in order], axis=1)

    branches = [place(chip, side) for chip in (0, 1) for side in (0, 1)]
    projected = lax.switch(half * 2 + core, branches, *candidates)
    layer_out = projected[None]
    return (layer_out, updated, moment_one, moment_two)


def solution(mesh):
    fine = Mesh(mesh.devices.reshape(4, 2, 4, 2, 2), DP + SEQ)
    data = P(DP, SEQ, None)
    blocks = P(DP, SEQ)
    in_specs = (data, data, data, P(), blocks, blocks, blocks, blocks)
    out_specs = (data, blocks, blocks, blocks)
    return jax.shard_map(
        on_device, mesh=fine, in_specs=in_specs, out_specs=out_specs, check_vma=False
    )
```

```python
import math

import jax
import jax.numpy as jnp
from jax import lax
from jax.sharding import Mesh, PartitionSpec as P

HEAD = 128
DP = ("z", "xl", "y")
SEQ = ("xh", "c")
H = 20
CH = 128


beta_one = 0.9
beta_two = 0.95
learn_rate = 0.0003
decay_rate = 0.1
adam_eps = 1e-08
step_count = 100
norm_eps = 1e-06


def ring_send(x, axis, size):
    if size == 2:
        return (lax.ppermute(x, axis, [(0, 1), (1, 0)]),)
    forward = [(k, (k + 1) % size) for k in range(size)]
    backward = [(k, (k - 1) % size) for k in range(size)]
    return (lax.ppermute(x, axis, forward), lax.ppermute(x, axis, backward))


def ring_far(received, axis, size):
    if size == 2:
        return received
    forward = [(k, (k + 1) % size) for k in range(size)]
    backward = [(k, (k - 1) % size) for k in range(size)]
    from_left, from_right = received
    half = from_left.shape[0] // 2
    far = jnp.concatenate(
        [
            lax.ppermute(from_left[:half], axis, forward),
            lax.ppermute(from_right[half:], axis, backward),
        ],
        axis=0,
    )
    return (from_left, far, from_right)


def ring_finish(x, received):
    return jnp.stack((x,) + tuple(received))


def ring_gather(x, axis, size):
    return ring_finish(x, ring_far(ring_send(x, axis, size), axis, size))


STAGES = (("y", "z"), ("z", "y"))


def ring_direct(x, axis, size):
    shifted = [
        lax.ppermute(x, axis, [(k, (k + shift) % size) for k in range(size)])
        for shift in (1, 2, 3)
    ]
    return jnp.stack([x] + shifted)


def gather_start(weights):
    near = swap(weights, "xl")
    peer = swap(weights, "xh")
    diagonal = lax.ppermute(weights, ("xl", "xh"), [(k, 3 - k) for k in range(4)])
    halves = (jnp.stack([weights, near]), jnp.stack([peer, diagonal]))
    return [ring_direct(part, first, 4) for part, (first, _) in zip(halves, STAGES)]


def gather_finish(parts, sent):
    z = lax.axis_index("z")
    xl = lax.axis_index("xl")
    y = lax.axis_index("y")
    stacked = jnp.arange(32)
    pieces = []
    for part, received, (first, _) in zip(parts, sent, STAGES):
        part = ring_finish(part, received)
        outer, inner, xl_rel = stacked // 8, (stacked // 2) % 4, stacked % 2
        z_rel, y_rel = (outer, inner) if first == "y" else (inner, outer)
        source = ((z - z_rel) % 4) * 8 + ((xl - xl_rel) % 2) * 4 + (y - y_rel) % 4
        pieces.append((part.reshape(-1, part.shape[-1]), source))
    return pieces


def seq_shift(x, shift):
    return lax.ppermute(x, SEQ, [(k, (k + shift) % 4) for k in range(4)])

def featurize(block, offset, seq_length):
    positions = (offset + jnp.arange(block.shape[0], dtype=jnp.int32)).astype(jnp.float32)
    angles = positions * (math.pi / (2.0 * seq_length))
    rectified = jnp.maximum(block.astype(jnp.float32), 0.0)
    cosine = rectified * jnp.cos(angles)[:, None, None]
    sine = rectified * jnp.sin(angles)[:, None, None]
    return jnp.concatenate([cosine, sine], axis=2).astype(jnp.bfloat16)


def to_blocks(x):
    return x.reshape((x.shape[0] // CH, CH) + x.shape[1:])


def normalize(attended, gain_rows):
    mean_square = jnp.mean(attended * attended, axis=2, keepdims=True)
    return (attended * lax.rsqrt(mean_square + norm_eps) * gain_rows[None]).astype(jnp.bfloat16)


def swap(x, axis):
    return lax.ppermute(x, axis, [(0, 1), (1, 0)])


def pair_exchange(x, core, keep_axis, join_axis):
    size = x.shape[keep_axis] // 2
    mine = lax.dynamic_slice_in_dim(x, core * size, size, keep_axis)
    theirs = lax.dynamic_slice_in_dim(x, (1 - core) * size, size, keep_axis)
    received = swap(theirs, "c")
    return lax.cond(
        core == 0,
        lambda a, b: jnp.concatenate([a, b], axis=join_axis),
        lambda a, b: jnp.concatenate([b, a], axis=join_axis),
        mine,
        received,
    )


def on_device(
    queries, keys_in, values_in, head_gain, master_weight, gradient, first_moment, second_moment
):
    moment_one = beta_one * first_moment + (1.0 - beta_one) * gradient
    moment_two = beta_two * second_moment + (1.0 - beta_two) * gradient * gradient
    corrected = (
        moment_one
        / (1.0 - beta_one**step_count)
        / (jnp.sqrt(moment_two / (1.0 - beta_two**step_count)) + adam_eps)
    )
    updated = master_weight - learn_rate * (corrected + decay_rate * master_weight)
    weights = updated.astype(jnp.bfloat16)
    tokens_here = queries.shape[1]
    seq_length = tokens_here * lax.axis_size(SEQ)
    half = lax.axis_index("xh")
    core = lax.axis_index("c")
    heads_here = H // 2
    parts = gather_start(weights)
    parts, query_heads = lax.optimization_barrier(
        (parts, queries[0].reshape(tokens_here, H, HEAD))
    )
    query_group = pair_exchange(query_heads, core, 1, 0)
    sent = [ring_send(part, second, 4) for part, (_, second) in zip(parts, STAGES)]
    key_group = pair_exchange(keys_in[0].reshape(tokens_here, H, HEAD), core, 1, 0)
    value_group = pair_exchange(values_in[0].reshape(tokens_here, H, HEAD), core, 1, 0)
    span = query_group.shape[0]
    offset = half * span
    query_blocks = to_blocks(featurize(query_group, offset, seq_length))
    key_blocks = to_blocks(featurize(key_group, offset, seq_length))
    value_blocks = to_blocks(value_group)
    states = jnp.einsum(
        "cjhf,cjhe->chfe", key_blocks, value_blocks, preferred_element_type=jnp.float32
    )
    chip_total = jnp.sum(states, axis=0)
    sent, chip_total = lax.optimization_barrier((sent, chip_total))
    sent = [ring_far(received, second, 4) for received, (_, second) in zip(sent, STAGES)]
    earlier = lax.ppermute(chip_total, "xh", [(0, 1)])
    scores = jnp.einsum(
        "cihf,cjhf->chij", query_blocks, key_blocks, preferred_element_type=jnp.float32
    )
    causal_mask = jnp.arange(CH)[:, None] >= jnp.arange(CH)[None, :]
    scores = jnp.where(causal_mask[None, None], scores, 0.0).astype(jnp.bfloat16)
    inside_block = jnp.einsum(
        "chij,cjhe->cihe", scores, value_blocks, preferred_element_type=jnp.float32
    )
    running = jnp.cumsum(states, axis=0)
    local_before = jnp.concatenate([jnp.zeros_like(states[:1]), running[:-1]], axis=0)
    before = (earlier[None] + local_before).astype(jnp.bfloat16)
    from_before = jnp.einsum(
        "cihf,chfe->cihe", query_blocks, before, preferred_element_type=jnp.float32
    )
    attended = (inside_block + from_before).reshape(span, heads_here, HEAD)
    sent, attended = lax.optimization_barrier((sent, attended))
    gain_rows = lax.dynamic_slice_in_dim(head_gain, core * heads_here, heads_here, 0)
    normed_group = normalize(attended, gain_rows)
    normed_own = pair_exchange(normed_group, core, 0, 1)
    normed_own = normed_own.reshape(tokens_here, H * HEAD)
    tokens = jnp.concatenate([normed_own, swap(normed_own, "c")], axis=0)
    by_block = tokens.reshape(tokens.shape[0], 32, -1)
    wide = []
    for rows, source in gather_finish(parts, sent):
        features = jnp.take(by_block, source, axis=1, mode="clip").reshape(tokens.shape)
        wide.append(
            jnp.dot(features, rows, preferred_element_type=jnp.float32).astype(jnp.bfloat16)
        )
    own = [piece[:tokens_here] for piece in wide]
    returned = [swap(piece[tokens_here:], "c") for piece in wide]
    candidates = own + returned

    def place(chip, side):
        order = []
        for block in range(4):
            from_partner = (block % 2 - side) % 2
            order.append(2 * from_partner + (block // 2 - chip) % 2)
        return lambda *pieces: jnp.concatenate([pieces[i] for i in order], axis=1)

    branches = [place(chip, side) for chip in (0, 1) for side in (0, 1)]
    projected = lax.switch(half * 2 + core, branches, *candidates)
    layer_out = projected[None]
    return (layer_out, updated, moment_one, moment_two)


def solution(mesh):
    fine = Mesh(mesh.devices.reshape(4, 2, 4, 2, 2), DP + SEQ)
    data = P(DP, SEQ, None)
    blocks = P(DP, SEQ)
    in_specs = (data, data, data, P(), blocks, blocks, blocks, blocks)
    out_specs = (data, blocks, blocks, blocks)
    return jax.shard_map(
        on_device, mesh=fine, in_specs=in_specs, out_specs=out_specs, check_vma=False
    )
```

```python
import math

import jax
import jax.numpy as jnp
from jax import lax
from jax.sharding import Mesh, PartitionSpec as P

HEAD = 128
DP = ("z", "xl", "y")
SEQ = ("xh", "c")
H = 20
CH = 128


beta_one = 0.9
beta_two = 0.95
learn_rate = 0.0003
decay_rate = 0.1
adam_eps = 1e-08
step_count = 100
norm_eps = 1e-06


def ring_send(x, axis, size):
    if size == 2:
        return (lax.ppermute(x, axis, [(0, 1), (1, 0)]),)
    forward = [(k, (k + 1) % size) for k in range(size)]
    backward = [(k, (k - 1) % size) for k in range(size)]
    return (lax.ppermute(x, axis, forward), lax.ppermute(x, axis, backward))


def ring_far(received, axis, size):
    if size == 2:
        return received
    forward = [(k, (k + 1) % size) for k in range(size)]
    backward = [(k, (k - 1) % size) for k in range(size)]
    from_left, from_right = received
    half = from_left.shape[0] // 2
    far = jnp.concatenate(
        [
            lax.ppermute(from_left[:half], axis, forward),
            lax.ppermute(from_right[half:], axis, backward),
        ],
        axis=0,
    )
    return (from_left, far, from_right)


def ring_finish(x, received):
    return jnp.stack((x,) + tuple(received))


def ring_gather(x, axis, size):
    return ring_finish(x, ring_far(ring_send(x, axis, size), axis, size))


STAGES = (("y", "z"), ("z", "y"))


def ring_direct(x, axis, size):
    shifted = [
        lax.ppermute(x, axis, [(k, (k + shift) % size) for k in range(size)])
        for shift in (1, 2, 3)
    ]
    return jnp.stack([x] + shifted)


def gather_start(weights):
    near = swap(weights, "xl")
    peer = swap(weights, "xh")
    diagonal = lax.ppermute(weights, ("xl", "xh"), [(k, 3 - k) for k in range(4)])
    halves = (jnp.stack([weights, near]), jnp.stack([peer, diagonal]))
    return [ring_direct(part, first, 4) for part, (first, _) in zip(halves, STAGES)]


def gather_finish(parts, sent):
    z = lax.axis_index("z")
    xl = lax.axis_index("xl")
    y = lax.axis_index("y")
    stacked = jnp.arange(32)
    pieces = []
    for part, received, (first, _) in zip(parts, sent, STAGES):
        part = ring_finish(part, received)
        outer, inner, xl_rel = stacked // 8, (stacked // 2) % 4, stacked % 2
        z_rel, y_rel = (outer, inner) if first == "y" else (inner, outer)
        source = ((z - z_rel) % 4) * 8 + ((xl - xl_rel) % 2) * 4 + (y - y_rel) % 4
        pieces.append((part.reshape(-1, part.shape[-1]), source))
    return pieces


def seq_shift(x, shift):
    return lax.ppermute(x, SEQ, [(k, (k + shift) % 4) for k in range(4)])

def featurize(block, offset, seq_length):
    positions = (offset + jnp.arange(block.shape[0], dtype=jnp.int32)).astype(jnp.float32)
    angles = positions * (math.pi / (2.0 * seq_length))
    rectified = jnp.maximum(block.astype(jnp.float32), 0.0)
    cosine = rectified * jnp.cos(angles)[:, None, None]
    sine = rectified * jnp.sin(angles)[:, None, None]
    return jnp.concatenate([cosine, sine], axis=2).astype(jnp.bfloat16)


def to_blocks(x):
    return x.reshape((x.shape[0] // CH, CH) + x.shape[1:])


def normalize(attended, gain_rows):
    mean_square = jnp.mean(attended * attended, axis=2, keepdims=True)
    return (attended * lax.rsqrt(mean_square + norm_eps) * gain_rows[None]).astype(jnp.bfloat16)


def swap(x, axis):
    return lax.ppermute(x, axis, [(0, 1), (1, 0)])


def pair_exchange(x, core, keep_axis, join_axis):
    size = x.shape[keep_axis] // 2
    mine = lax.dynamic_slice_in_dim(x, core * size, size, keep_axis)
    theirs = lax.dynamic_slice_in_dim(x, (1 - core) * size, size, keep_axis)
    received = swap(theirs, "c")
    return jnp.where(
        core == 0,
        jnp.concatenate([mine, received], axis=join_axis),
        jnp.concatenate([received, mine], axis=join_axis),
    )


def on_device(
    queries, keys_in, values_in, head_gain, master_weight, gradient, first_moment, second_moment
):
    moment_one = beta_one * first_moment + (1.0 - beta_one) * gradient
    moment_two = beta_two * second_moment + (1.0 - beta_two) * gradient * gradient
    corrected = (
        moment_one
        / (1.0 - beta_one**step_count)
        / (jnp.sqrt(moment_two / (1.0 - beta_two**step_count)) + adam_eps)
    )
    updated = master_weight - learn_rate * (corrected + decay_rate * master_weight)
    weights = updated.astype(jnp.bfloat16)
    tokens_here = queries.shape[1]
    seq_length = tokens_here * lax.axis_size(SEQ)
    half = lax.axis_index("xh")
    core = lax.axis_index("c")
    heads_here = H // 2
    parts = gather_start(weights)
    parts, query_heads = lax.optimization_barrier(
        (parts, queries[0].reshape(tokens_here, H, HEAD))
    )
    query_group = pair_exchange(query_heads, core, 1, 0)
    sent = [ring_send(part, second, 4) for part, (_, second) in zip(parts, STAGES)]
    key_group = pair_exchange(keys_in[0].reshape(tokens_here, H, HEAD), core, 1, 0)
    value_group = pair_exchange(values_in[0].reshape(tokens_here, H, HEAD), core, 1, 0)
    span = query_group.shape[0]
    offset = half * span
    query_blocks = to_blocks(featurize(query_group, offset, seq_length))
    key_blocks = to_blocks(featurize(key_group, offset, seq_length))
    value_blocks = to_blocks(value_group)
    states = jnp.einsum(
        "cjhf,cjhe->chfe", key_blocks, value_blocks, preferred_element_type=jnp.float32
    )
    chip_total = jnp.sum(states, axis=0)
    sent, chip_total = lax.optimization_barrier((sent, chip_total))
    sent = [ring_far(received, second, 4) for received, (_, second) in zip(sent, STAGES)]
    earlier = lax.ppermute(chip_total, "xh", [(0, 1)])
    scores = jnp.einsum(
        "cihf,cjhf->chij", query_blocks, key_blocks, preferred_element_type=jnp.float32
    )
    causal_mask = jnp.arange(CH)[:, None] >= jnp.arange(CH)[None, :]
    scores = jnp.where(causal_mask[None, None], scores, 0.0).astype(jnp.bfloat16)
    inside_block = jnp.einsum(
        "chij,cjhe->cihe", scores, value_blocks, preferred_element_type=jnp.float32
    )
    running = jnp.cumsum(states, axis=0)
    local_before = jnp.concatenate([jnp.zeros_like(states[:1]), running[:-1]], axis=0)
    before = (earlier[None] + local_before).astype(jnp.bfloat16)
    from_before = jnp.einsum(
        "cihf,chfe->cihe", query_blocks, before, preferred_element_type=jnp.float32
    )
    attended = (inside_block + from_before).reshape(span, heads_here, HEAD)
    sent, attended = lax.optimization_barrier((sent, attended))
    gain_rows = lax.dynamic_slice_in_dim(head_gain, core * heads_here, heads_here, 0)
    normed_group = normalize(attended, gain_rows)
    other_heads = swap(normed_group, "c")
    tokens = jnp.where(
        core == 0,
        jnp.concatenate([normed_group, other_heads], axis=1),
        jnp.concatenate([other_heads, normed_group], axis=1),
    ).reshape(span, H * HEAD)
    by_block = tokens.reshape(tokens.shape[0], 32, -1)
    wide = []
    for rows, source in gather_finish(parts, sent):
        features = jnp.take(by_block, source, axis=1, mode="clip").reshape(tokens.shape)
        wide.append(
            jnp.dot(features, rows, preferred_element_type=jnp.float32).astype(jnp.bfloat16)
        )
    own = [lax.dynamic_slice_in_dim(piece, core * tokens_here, tokens_here, 0) for piece in wide]
    returned = [
        swap(lax.dynamic_slice_in_dim(piece, (1 - core) * tokens_here, tokens_here, 0), "c")
        for piece in wide
    ]
    candidates = own + returned

    def place(chip, side):
        order = []
        for block in range(4):
            from_partner = (block % 2 - side) % 2
            order.append(2 * from_partner + (block // 2 - chip) % 2)
        return lambda *pieces: jnp.concatenate([pieces[i] for i in order], axis=1)

    branches = [place(chip, side) for chip in (0, 1) for side in (0, 1)]
    projected = lax.switch(half * 2 + core, branches, *candidates)
    layer_out = projected[None]
    return (layer_out, updated, moment_one, moment_two)


def solution(mesh):
    fine = Mesh(mesh.devices.reshape(4, 2, 4, 2, 2), DP + SEQ)
    data = P(DP, SEQ, None)
    blocks = P(DP, SEQ)
    in_specs = (data, data, data, P(), blocks, blocks, blocks, blocks)
    out_specs = (data, blocks, blocks, blocks)
    return jax.shard_map(
        on_device, mesh=fine, in_specs=in_specs, out_specs=out_specs, check_vma=False
    )
```
